512 devices in a mesh: space: 64 (over z_lo, y, core), chan: 8 (over x, z_hi).
Axes of the slice: x: 4, y: 8, z: 8 (z_hi: 2, z_lo: 4; z = z_hi * 4 + z_lo), core: 2. Of those that a mesh axis runs over, the one named last changes fastest.
Arguments:
- features: bfloat16 [1, 128, 128, 2048], P(None, 'chan', 'space'), may hold values from -6 to 6
- top_map: int32 [64, 2048], P('space'), may hold values from 0 to 2048, as said below
- bottom_map: int32 [64, 2048], P('space'), may hold values from 0 to 2048, as said below
- first_weight: bfloat16 [128, 3, 3, 128], P('chan'), may hold values from -0.1875 to 0.1875
- first_bias: float32 [128], P('chan'), may hold values from -3 to 3
- second_weight: bfloat16 [256, 3, 3, 128], P('chan'), may hold values from -0.1875 to 0.1875
- second_bias: float32 [256], P('chan'), may hold values from -3 to 3
Outputs:
- hidden: bfloat16 [1, 128, 128, 2048], P(None, 'chan', 'space')
- coarse: bfloat16 [1, 256, 64, 1024], P(None, 'chan', 'space')
The draws below stay inside these ranges and needn't reach their ends.
Inputs may be any that keep to these rules, and one draw needn't show every extreme that they name: `top_map`: each entry of row s, column k is k - 1, k or k + 1 taken modulo 2048, or 2048 for a missing neighbour at a face corner; exactly 4 entries of each row equal 2048. `bottom_map`: each entry of row s, column k is k - 1, k or k + 1 taken modulo 2048, or 2048 for a missing neighbour at a face corner; exactly 4 entries of each row equal 2048.
All inputs are finite; a program needn't handle non-finite values.
Results may differ from the reference program's by a relative error of at most 0.012.
Values may be sent and summed in bfloat16 or wider, within the bound.
No kernel may reach another device: no remote copies, remote signals or barrier semaphores. Data moves between devices by JAX's collectives and lax.ppermute only.
A program may use at most 64 MiB of HBM per device.

```python
from functools import partial
import jax
import jax.numpy as jnp
from jax import lax

C = 128
C2 = 256
CYCLE = 2048
MEMBERS = 1
TILES = 64
CYCLES = 128


def corner_columns(corner_key):
    return jax.random.permutation(corner_key, CYCLE)[:4]


def rim_table(key):
    shift_key, corner_key = jax.random.split(key)
    shifts = jax.random.randint(shift_key, (TILES, CYCLE), -1, 2)
    columns = (jnp.arange(CYCLE)[None, :] + shifts) % CYCLE
    corner_keys = jax.random.split(corner_key, TILES)
    corners = jax.vmap(corner_columns)(corner_keys)
    marked = jnp.any(jnp.arange(CYCLE)[None, None, :] == corners[:, :, None], axis=1)
    return jnp.where(marked, CYCLE, columns).astype(jnp.int32)


def draw_top_map(key, part):
    return rim_table(jax.random.fold_in(key, 11))


def draw_bottom_map(key, part):
    return rim_table(jax.random.fold_in(key, 23))


def shard_levels(own_key, dims, pieces, least, top_value):
    gain = 1.0
    for dim, shards_of in pieces:
        steps = jax.random.uniform(jax.random.fold_in(jax.random.fold_in(own_key, 6), dim), (shards_of,), jnp.float32, least / len(pieces), top_value / len(pieces))
        gain = gain * jnp.repeat(jnp.exp(steps), dims[dim] // shards_of).reshape((-1,) + (1,) * (len(dims) - 1 - dim))
    return gain


def centred(stream_key, shape, spread, reach, pieces=(), held_as=jnp.bfloat16):
    drawn = spread * jax.random.normal(stream_key, shape, jnp.float32)
    if pieces:
        drawn = drawn * shard_levels(stream_key, shape, pieces, -0.22, 0.18)
    return jnp.clip(drawn, -reach, reach).astype(held_as)


def setup_inputs(seed: int = 0) -> dict:
    key_of = jax.random.split(jax.random.key(seed), 8)
    features = centred(key_of[0], (MEMBERS, C, CYCLES, CYCLE), 1.0, 6.0, ((1, 8), (2, 64)))
    top_map = draw_top_map(jax.random.fold_in(key_of[7], 71), 0)
    bottom_map = draw_bottom_map(jax.random.fold_in(key_of[7], 71), 0)
    first_weight = centred(key_of[3], (C, 3, 3, C), (9 * C) ** -0.5, 0.1875, ((0, 8),))
    first_bias = centred(key_of[4], (C,), 0.5, 3.0, ((0, 8),), jnp.float32)
    second_weight = centred(key_of[5], (C2, 3, 3, C), (9 * C) ** -0.5, 0.1875, ((0, 8),))
    second_bias = centred(key_of[6], (C2,), 0.5, 3.0, ((0, 8),), jnp.float32)
    return {"features": features, "top_map": top_map, "bottom_map": bottom_map, "first_weight": first_weight, "first_bias": first_bias, "second_weight": second_weight, "second_bias": second_bias}


def remap_rows(source_rows, table):
    zero_col = jnp.zeros(source_rows.shape[:-1] + (1,), source_rows.dtype)
    extended = jnp.concatenate([source_rows, zero_col], axis=-1)
    index = jnp.broadcast_to(table, source_rows.shape).astype(jnp.int32)
    return jnp.take_along_axis(extended, index, axis=-1)


def first_layer(sample, top_map, bottom_map, first_weight, first_bias):
    channels, cycle_count, cycle_width = sample.shape
    tile_count = top_map.shape[0]
    per_tile = cycle_count // tile_count
    band_rows = sample.reshape(channels, tile_count, per_tile, cycle_width)
    zero_row = jnp.zeros((channels, 1, cycle_width), sample.dtype)
    above_row = remap_rows(jnp.concatenate([zero_row, band_rows[:, :-1, -1, :]], 1), top_map)
    below_row = remap_rows(jnp.concatenate([band_rows[:, 1:, 0, :], zero_row], 1), bottom_map)
    padded = jnp.concatenate([above_row[:, :, None], band_rows, below_row[:, :, None]], 2).astype(jnp.float32)
    weight = first_weight.astype(jnp.float32)
    totals = jnp.zeros((weight.shape[0], tile_count, per_tile, cycle_width), jnp.float32)
    for row_step in range(3):
        for col_step in range(3):
            shifted = jnp.roll(padded[:, :, row_step:row_step + per_tile, :], 1 - col_step, axis=3)
            totals = totals + jnp.einsum("oc,csrw->osrw", weight[:, row_step, col_step, :], shifted)
    result = jax.nn.gelu(totals + first_bias.astype(jnp.float32)[:, None, None, None]).astype(jnp.bfloat16)
    return result.reshape(-1, cycle_count, cycle_width)


def second_layer(sample, top_map, second_weight, second_bias):
    channels, cycle_count, cycle_width = sample.shape
    tile_count = top_map.shape[0]
    per_tile = cycle_count // tile_count
    band_rows = sample.reshape(channels, tile_count, per_tile, cycle_width)
    zero_row = jnp.zeros((channels, 1, cycle_width), sample.dtype)
    above_row = remap_rows(jnp.concatenate([zero_row, band_rows[:, :-1, -1, :]], 1), top_map)
    stacked = jnp.concatenate([above_row[:, :, None], band_rows], 2).astype(jnp.float32)
    weight = second_weight.astype(jnp.float32)
    totals = jnp.zeros((weight.shape[0], tile_count, per_tile // 2, cycle_width // 2), jnp.float32)
    for row_step in range(3):
        for col_step in range(3):
            picked = jnp.roll(stacked[:, :, row_step:row_step + per_tile:2, :], 1 - col_step, axis=3)[..., ::2]
            totals = totals + jnp.einsum("oc,csrw->osrw", weight[:, row_step, col_step, :], picked)
    result = jax.nn.gelu(totals + second_bias.astype(jnp.float32)[:, None, None, None]).astype(jnp.bfloat16)
    return result.reshape(-1, cycle_count // 2, cycle_width // 2)


def reference(features, top_map, bottom_map, first_weight, first_bias, second_weight, second_bias):
    hidden = lax.map(partial(first_layer, top_map=top_map, bottom_map=bottom_map, first_weight=first_weight, first_bias=first_bias), features)
    coarse = lax.map(partial(second_layer, top_map=top_map, second_weight=second_weight, second_bias=second_bias), hidden)
    return (hidden, coarse)
```

```python
import jax
import jax.numpy as jnp
from jax import lax
from jax.sharding import PartitionSpec as P


def shifted(array, axis, by):
    devices = lax.axis_size(axis)
    pairs = [(i, i + by) for i in range(devices) if 0 <= i + by < devices]
    return lax.ppermute(array, axis, pairs)


def remap_window(source, table, first_col, width):
    cycle = table.shape[0]
    cols = (first_col + jnp.arange(width)) % cycle
    picked = lax.dynamic_slice_in_dim(
        jnp.concatenate([table, table], axis=0), first_col % cycle, width, axis=0
    )
    same = source[..., 1 : width + 1]
    prev = source[..., 0:width]
    nxt = source[..., 2 : width + 2]
    zero = jnp.zeros_like(same)
    out = jnp.where(picked == (cols + cycle - 1) % cycle, prev, zero)
    out = jnp.where(picked == (cols + 1) % cycle, nxt, out)
    out = jnp.where(picked == cols, same, out)
    return out


def remap_full(row, table):
    cycle = table.shape[0]
    wrapped = jnp.concatenate([row[..., -1:], row, row[..., :1]], axis=-1)
    return remap_window(wrapped, table, 0, cycle)


def conv(x, w, stride):
    return lax.conv_general_dilated(
        x,
        w,
        window_strides=stride,
        padding="VALID",
        dimension_numbers=("NCHW", "OHWI", "NCHW"),
        preferred_element_type=jnp.float32,
    )


def per_device(features, top_map, bottom_map, first_weight, first_bias, second_weight, second_bias):
    groups = lax.axis_size("chan")
    me = lax.axis_index("chan")
    x = features[0]
    rows = x.shape[1]
    cycle = x.shape[2]
    block = cycle // groups
    upper_map = top_map[0]
    lower_map = bottom_map[0]

    w1 = lax.all_gather(first_weight, "chan", axis=0, tiled=True)
    b1 = lax.all_gather(first_bias, "chan", axis=0, tiled=True)
    w2 = lax.all_gather(second_weight, "chan", axis=0, tiled=True)
    b2 = lax.all_gather(second_bias, "chan", axis=0, tiled=True)

    above_src = shifted(x[:, rows - 1, :], "space", 1)
    below_src = shifted(x[:, 0, :], "space", -1)
    above = remap_full(above_src, upper_map)
    below = remap_full(below_src, lower_map)
    padded = jnp.concatenate([above[:, None], x, below[:, None]], axis=1)

    halo = 3
    width = block + 2 * halo
    ext = jnp.concatenate([padded[..., cycle - halo :], padded, padded[..., :halo]], axis=-1)
    sends = jnp.stack([ext[..., j * block : j * block + width] for j in range(groups)], 0)
    got = lax.all_to_all(sends, "chan", 0, 0, tiled=True)
    window = got.reshape((-1,) + got.shape[2:])

    pre1 = conv(window[None], w1, (1, 1))
    hidden_win = jax.nn.gelu(pre1 + b1[None, :, None, None]).astype(jnp.bfloat16)[0]

    hidden_out = lax.all_to_all(
        hidden_win[:, :, halo - 1 : halo - 1 + block], "chan", 0, 2, tiled=True
    )

    rim_src = shifted(hidden_win[:, rows - 1, :], "space", 1)
    rim = remap_window(rim_src, upper_map, me * block - 1, block + 2)
    stacked = jnp.concatenate([rim[:, None], hidden_win[:, :, 1 : block + 3]], axis=1)
    pre2 = conv(stacked[None], w2, (1, 2))
    coarse_win = jax.nn.gelu(pre2 + b2[None, :, None, None]).astype(jnp.bfloat16)[0]
    coarse_out = lax.all_to_all(coarse_win, "chan", 0, 2, tiled=True)
    return hidden_out[None], coarse_out[None]


def solution(mesh):
    placed = (
        P(None, "chan", "space", None),
        P("space", None),
        P("space", None),
        P("chan", None, None, None),
        P("chan"),
        P("chan", None, None, None),
        P("chan"),
    )
    return jax.shard_map(
        per_device,
        mesh=mesh,
        in_specs=placed,
        out_specs=(P(None, "chan", "space", None), P(None, "chan", "space", None)),
        check_vma=False,
    )
```

```python
import jax
import jax.numpy as jnp
from jax import lax
from jax.sharding import PartitionSpec as P


def shifted(array, axis, by):
    devices = lax.axis_size(axis)
    pairs = [(i, i + by) for i in range(devices) if 0 <= i + by < devices]
    return lax.ppermute(array, axis, pairs)


def remap_window(source, table, first_col, width):
    cycle = table.shape[0]
    cols = (first_col + jnp.arange(width)) % cycle
    picked = lax.dynamic_slice_in_dim(
        jnp.concatenate([table, table], axis=0), first_col % cycle, width, axis=0
    )
    same = source[..., 1 : width + 1]
    prev = source[..., 0:width]
    nxt = source[..., 2 : width + 2]
    zero = jnp.zeros_like(same)
    out = jnp.where(picked == (cols + cycle - 1) % cycle, prev, zero)
    out = jnp.where(picked == (cols + 1) % cycle, nxt, out)
    out = jnp.where(picked == cols, same, out)
    return out


def remap_full(row, table):
    cycle = table.shape[0]
    wrapped = jnp.concatenate([row[..., -1:], row, row[..., :1]], axis=-1)
    return remap_window(wrapped, table, 0, cycle)


def gather_chan(x):
    groups = lax.axis_size("chan")
    me = lax.axis_index("chan")
    got = [x]
    for k in range(1, groups):
        pairs = [(i, (i + k) % groups) for i in range(groups)]
        got.append(lax.ppermute(x, "chan", pairs))
    ahead = jnp.stack([got[0]] + got[:0:-1], 0)
    both = jnp.concatenate([ahead, ahead], 0)
    ordered = lax.dynamic_slice_in_dim(both, (groups - me) % groups, groups, axis=0)
    return ordered.reshape((-1,) + x.shape[1:])


def split3(v):
    hi = v.astype(jnp.bfloat16)
    rest = v - hi.astype(jnp.float32)
    mid = rest.astype(jnp.bfloat16)
    lo = (rest - mid.astype(jnp.float32)).astype(jnp.bfloat16)
    return jnp.stack([hi, mid, lo], -1)


def join3(parts):
    parts = parts.astype(jnp.float32)
    return (parts[..., 0] + parts[..., 1]) + parts[..., 2]


def conv(x, w, stride):
    return lax.conv_general_dilated(
        x,
        w,
        window_strides=stride,
        padding="VALID",
        dimension_numbers=("NCHW", "OHWI", "NCHW"),
        preferred_element_type=jnp.float32,
    )


def per_device(features, top_map, bottom_map, first_weight, first_bias, second_weight, second_bias):
    groups = lax.axis_size("chan")
    me = lax.axis_index("chan")
    x = features[0]
    rows = x.shape[1]
    cycle = x.shape[2]
    block = cycle // groups
    upper_map = top_map[0]
    lower_map = bottom_map[0]

    n1 = first_weight.shape[0]
    n2 = second_weight.shape[0]
    flat = jnp.concatenate(
        [first_weight.reshape(n1, -1), second_weight.reshape(n2, -1)], axis=0
    )
    packed = jnp.concatenate(
        [flat, split3(jnp.concatenate([first_bias, second_bias]))], axis=1
    )
    every = gather_chan(packed[None]).reshape((groups, n1 + n2, -1))
    taps = flat.shape[1]
    w1 = every[:, :n1, :taps].reshape((-1,) + first_weight.shape[1:])
    w2 = every[:, n1:, :taps].reshape((-1,) + second_weight.shape[1:])
    b1 = join3(every[:, :n1, taps:]).reshape(-1)
    b2 = join3(every[:, n1:, taps:]).reshape(-1)

    above_src = shifted(x[:, rows - 1, :], "space", 1)
    below_src = shifted(x[:, 0, :], "space", -1)
    above = remap_full(above_src, upper_map)
    below = remap_full(below_src, lower_map)
    padded = jnp.concatenate([above[:, None], x, below[:, None]], axis=1)

    halo = 3
    width = block + 2 * halo
    ext = jnp.concatenate([padded[..., cycle - halo :], padded, padded[..., :halo]], axis=-1)
    sends = jnp.stack([ext[..., j * block : j * block + width] for j in range(groups)], 0)
    got = lax.all_to_all(sends, "chan", 0, 0, tiled=True)
    window = got.reshape((-1,) + got.shape[2:])

    pre1 = conv(window[None], w1, (1, 1))
    hidden_win = jax.nn.gelu(pre1 + b1[None, :, None, None]).astype(jnp.bfloat16)[0]

    hidden_out = lax.all_to_all(
        hidden_win[:, :, halo - 1 : halo - 1 + block], "chan", 0, 2, tiled=True
    )

    rim_src = shifted(hidden_win[:, rows - 1, :], "space", 1)
    rim = remap_window(rim_src, upper_map, me * block - 1, block + 2)
    stacked = jnp.concatenate([rim[:, None], hidden_win[:, :, 1 : block + 3]], axis=1)
    pre2 = conv(stacked[None], w2, (1, 2))
    coarse_win = jax.nn.gelu(pre2 + b2[None, :, None, None]).astype(jnp.bfloat16)[0]
    coarse_out = lax.all_to_all(coarse_win, "chan", 0, 2, tiled=True)
    return hidden_out[None], coarse_out[None]


def solution(mesh):
    placed = (
        P(None, "chan", "space", None),
        P("space", None),
        P("space", None),
        P("chan", None, None, None),
        P("chan"),
        P("chan", None, None, None),
        P("chan"),
    )
    return jax.shard_map(
        per_device,
        mesh=mesh,
        in_specs=placed,
        out_specs=(P(None, "chan", "space", None), P(None, "chan", "space", None)),
        check_vma=False,
    )
```

```python
import jax
import jax.numpy as jnp
from jax import lax
from jax.sharding import PartitionSpec as P


def shifted(array, axis, by):
    devices = lax.axis_size(axis)
    pairs = [(i, i + by) for i in range(devices) if 0 <= i + by < devices]
    return lax.ppermute(array, axis, pairs)


def remap_window(source, table, first_col, width):
    cycle = table.shape[0]
    cols = (first_col + jnp.arange(width)) % cycle
    picked = lax.dynamic_slice_in_dim(
        jnp.concatenate([table, table], axis=0), first_col % cycle, width, axis=0
    )
    same = source[..., 1 : width + 1]
    prev = source[..., 0:width]
    nxt = source[..., 2 : width + 2]
    zero = jnp.zeros_like(same)
    out = jnp.where(picked == (cols + cycle - 1) % cycle, prev, zero)
    out = jnp.where(picked == (cols + 1) % cycle, nxt, out)
    out = jnp.where(picked == cols, same, out)
    return out


def remap_full(row, table):
    cycle = table.shape[0]
    wrapped = jnp.concatenate([row[..., -1:], row, row[..., :1]], axis=-1)
    return remap_window(wrapped, table, 0, cycle)


def split3(v):
    hi = lax.reduce_precision(v, exponent_bits=8, mantissa_bits=7)
    rest = v - hi
    mid = lax.reduce_precision(rest, exponent_bits=8, mantissa_bits=7)
    lo = rest - mid
    return jnp.stack([hi, mid, lo], -1).astype(jnp.bfloat16)


def join3(parts):
    parts = parts.astype(jnp.float32)
    return (parts[..., 0] + parts[..., 1]) + parts[..., 2]


def conv(x, w, stride):
    return lax.conv_general_dilated(
        x,
        w,
        window_strides=stride,
        padding="VALID",
        dimension_numbers=("NCHW", "OHWI", "NCHW"),
        preferred_element_type=jnp.float32,
    )


def column_windows(padded, groups, halo):
    cycle = padded.shape[-1]
    block = cycle // groups
    lead = padded.shape[:-1]
    left = jnp.roll(padded, halo, axis=-1).reshape(lead + (groups, block))[..., :halo]
    mid = padded.reshape(lead + (groups, block))
    right = jnp.roll(padded, -halo, axis=-1).reshape(lead + (groups, block))[..., block - halo :]
    wins = jnp.concatenate([left, mid, right], axis=-1)
    return jnp.moveaxis(wins, -2, 0)


def pad_to(flat, multiple):
    extra = (-flat.shape[-1]) % multiple
    return jnp.pad(flat, [(0, 0)] * (flat.ndim - 1) + [(0, extra)])


def per_device(features, top_map, bottom_map, first_weight, first_bias, second_weight, second_bias):
    groups = lax.axis_size("chan")
    me = lax.axis_index("chan")
    x = features[0]
    chans = x.shape[0]
    rows = x.shape[1]
    cycle = x.shape[2]
    block = cycle // groups
    upper_map = top_map[0]
    lower_map = bottom_map[0]
    n1 = first_weight.shape[0]
    n2 = second_weight.shape[0]

    above_src = shifted(x[:, rows - 1, :], "space", 1)
    below_src = shifted(x[:, 0, :], "space", -1)
    above = remap_full(above_src, upper_map)
    below = remap_full(below_src, lower_map)
    padded = jnp.concatenate([above[:, None], x, below[:, None]], axis=1)

    halo = 3
    width = block + 2 * halo
    wins = column_windows(padded, groups, halo).reshape(groups, -1)
    feat_len = wins.shape[1]

    flat_w = jnp.concatenate(
        [first_weight.reshape(n1, -1), second_weight.reshape(n2, -1)], axis=0
    )
    taps = flat_w.shape[1]
    packed_w = jnp.concatenate(
        [flat_w, split3(jnp.concatenate([first_bias, second_bias]))], axis=1
    ).reshape(1, -1)
    sends = jnp.concatenate([wins, jnp.broadcast_to(packed_w, (groups,) + packed_w.shape[1:])], 1)
    got = lax.all_to_all(pad_to(sends, 1024), "chan", 0, 0, tiled=True)

    window = got[:, :feat_len].reshape(groups * chans, rows + 2, width)
    every = got[:, feat_len : feat_len + packed_w.shape[1]].reshape(groups, n1 + n2, taps + 3)
    w1 = every[:, :n1, :taps].reshape((-1,) + first_weight.shape[1:])
    w2 = every[:, n1:, :taps].reshape((-1,) + second_weight.shape[1:])
    b1 = join3(every[:, :n1, taps:]).reshape(-1)
    b2 = join3(every[:, n1:, taps:]).reshape(-1)

    pre1 = conv(window[None], w1, (1, 1))
    hidden_win = jax.nn.gelu(pre1 + b1[None, :, None, None]).astype(jnp.bfloat16)[0]

    rim_src = shifted(hidden_win[:, rows - 1, :], "space", 1)
    rim = remap_window(rim_src, upper_map, me * block - 1, block + 2)
    stacked = jnp.concatenate([rim[:, None], hidden_win[:, :, 1 : block + 3]], axis=1)
    pre2 = conv(stacked[None], w2, (1, 2))
    coarse_win = jax.nn.gelu(pre2 + b2[None, :, None, None]).astype(jnp.bfloat16)[0]

    hidden_part = hidden_win[:, :, halo - 1 : halo - 1 + block].reshape(groups, -1)
    coarse_part = coarse_win.reshape(groups, -1)
    back = lax.all_to_all(
        jnp.concatenate([hidden_part, coarse_part], 1), "chan", 0, 0, tiled=True
    )
    h_len = hidden_part.shape[1]
    hidden_out = back[:, :h_len].reshape((groups, chans, rows, block))
    hidden_out = jnp.moveaxis(hidden_out, 0, 2).reshape(chans, rows, cycle)
    coarse_shape = coarse_win.shape
    coarse_out = back[:, h_len:].reshape(
        (groups, coarse_shape[0] // groups) + coarse_shape[1:]
    )
    coarse_out = jnp.moveaxis(coarse_out, 0, 2).reshape(
        (coarse_shape[0] // groups, coarse_shape[1], groups * coarse_shape[2])
    )
    return hidden_out[None], coarse_out[None]


def solution(mesh):
    placed = (
        P(None, "chan", "space", None),
        P("space", None),
        P("space", None),
        P("chan", None, None, None),
        P("chan"),
        P("chan", None, None, None),
        P("chan"),
    )
    return jax.shard_map(
        per_device,
        mesh=mesh,
        in_specs=placed,
        out_specs=(P(None, "chan", "space", None), P(None, "chan", "space", None)),
        check_vma=False,
    )
```

```python
import jax
import jax.numpy as jnp
from jax import lax
from jax.sharding import PartitionSpec as P


def shifted(array, axis, by):
    devices = lax.axis_size(axis)
    pairs = [(i, i + by) for i in range(devices) if 0 <= i + by < devices]
    return lax.ppermute(array, axis, pairs)


def remap_window(source, table, first_col, width):
    cycle = table.shape[0]
    cols = (first_col + jnp.arange(width)) % cycle
    picked = lax.dynamic_slice_in_dim(
        jnp.concatenate([table, table], axis=0), first_col % cycle, width, axis=0
    )
    same = source[..., 1 : width + 1]
    prev = source[..., 0:width]
    nxt = source[..., 2 : width + 2]
    zero = jnp.zeros_like(same)
    out = jnp.where(picked == (cols + cycle - 1) % cycle, prev, zero)
    out = jnp.where(picked == (cols + 1) % cycle, nxt, out)
    out = jnp.where(picked == cols, same, out)
    return out


def remap_full(row, table):
    cycle = table.shape[0]
    wrapped = jnp.concatenate([row[..., -1:], row, row[..., :1]], axis=-1)
    return remap_window(wrapped, table, 0, cycle)


def split3(v):
    hi = lax.reduce_precision(v, exponent_bits=8, mantissa_bits=7)
    rest = v - hi
    mid = lax.reduce_precision(rest, exponent_bits=8, mantissa_bits=7)
    lo = rest - mid
    return jnp.stack([hi, mid, lo], -1).astype(jnp.bfloat16)


def join3(parts):
    parts = parts.astype(jnp.float32)
    return (parts[..., 0] + parts[..., 1]) + parts[..., 2]


def conv(x, w, stride):
    return lax.conv_general_dilated(
        x,
        w,
        window_strides=stride,
        padding="VALID",
        dimension_numbers=("NCHW", "OHWI", "NCHW"),
        preferred_element_type=jnp.float32,
    )


def column_windows(padded, groups, halo):
    cycle = padded.shape[-1]
    block = cycle // groups
    lead = padded.shape[:-1]
    left = jnp.roll(padded, halo, axis=-1).reshape(lead + (groups, block))[..., :halo]
    mid = padded.reshape(lead + (groups, block))
    right = jnp.roll(padded, -halo, axis=-1).reshape(lead + (groups, block))[..., block - halo :]
    wins = jnp.concatenate([left, mid, right], axis=-1)
    return jnp.moveaxis(wins, -2, 0)


def pad_to(flat, multiple):
    extra = (-flat.shape[-1]) % multiple
    return jnp.pad(flat, [(0, 0)] * (flat.ndim - 1) + [(0, extra)])


def per_device(features, top_map, bottom_map, first_weight, first_bias, second_weight, second_bias):
    groups = lax.axis_size("chan")
    me = lax.axis_index("chan")
    x = features[0]
    chans = x.shape[0]
    rows = x.shape[1]
    cycle = x.shape[2]
    block = cycle // groups
    upper_map = top_map[0]
    lower_map = bottom_map[0]
    n1 = first_weight.shape[0]
    n2 = second_weight.shape[0]

    halo = 3
    width = block + 2 * halo
    wins = column_windows(x, groups, halo + 1).reshape(groups, -1)
    feat_len = wins.shape[1]

    flat_w = jnp.concatenate(
        [first_weight.reshape(n1, -1), second_weight.reshape(n2, -1)], axis=0
    )
    taps = flat_w.shape[1]
    packed_w = jnp.concatenate(
        [flat_w, split3(jnp.concatenate([first_bias, second_bias]))], axis=1
    ).reshape(1, -1)
    sends = jnp.concatenate([wins, jnp.broadcast_to(packed_w, (groups,) + packed_w.shape[1:])], 1)
    got = lax.all_to_all(pad_to(sends, 1024), "chan", 0, 0, tiled=True)

    tile = got[:, :feat_len].reshape(groups * chans, rows, width + 2)
    every = got[:, feat_len : feat_len + packed_w.shape[1]].reshape(groups, n1 + n2, taps + 3)
    w1 = every[:, :n1, :taps].reshape((-1,) + first_weight.shape[1:])
    w2 = every[:, n1:, :taps].reshape((-1,) + second_weight.shape[1:])
    b1 = join3(every[:, :n1, taps:]).reshape(-1)
    b2 = join3(every[:, n1:, taps:]).reshape(-1)

    above_src = shifted(tile[:, rows - 1, :], "space", 1)
    below_src = shifted(tile[:, 0, :], "space", -1)
    above = remap_window(above_src, upper_map, me * block - halo, width)
    below = remap_window(below_src, lower_map, me * block - halo, width)
    window = jnp.concatenate([above[:, None], tile[:, :, 1 : width + 1], below[:, None]], axis=1)

    pre1 = conv(window[None], w1, (1, 1))
    hidden_win = jax.nn.gelu(pre1 + b1[None, :, None, None]).astype(jnp.bfloat16)[0]

    rim_src = shifted(hidden_win[:, rows - 1, :], "space", 1)
    rim = remap_window(rim_src, upper_map, me * block - 1, block + 2)
    stacked = jnp.concatenate([rim[:, None], hidden_win[:, :, 1 : block + 3]], axis=1)
    pre2 = conv(stacked[None], w2, (1, 2))
    coarse_win = jax.nn.gelu(pre2 + b2[None, :, None, None]).astype(jnp.bfloat16)[0]

    hidden_part = hidden_win[:, :, halo - 1 : halo - 1 + block].reshape(groups, -1)
    coarse_part = coarse_win.reshape(groups, -1)
    back = lax.all_to_all(
        jnp.concatenate([hidden_part, coarse_part], 1), "chan", 0, 0, tiled=True
    )
    h_len = hidden_part.shape[1]
    hidden_out = back[:, :h_len].reshape((groups, chans, rows, block))
    hidden_out = jnp.moveaxis(hidden_out, 0, 2).reshape(chans, rows, cycle)
    coarse_shape = coarse_win.shape
    coarse_out = back[:, h_len:].reshape(
        (groups, coarse_shape[0] // groups) + coarse_shape[1:]
    )
    coarse_out = jnp.moveaxis(coarse_out, 0, 2).reshape(
        (coarse_shape[0] // groups, coarse_shape[1], groups * coarse_shape[2])
    )
    return hidden_out[None], coarse_out[None]


def solution(mesh):
    placed = (
        P(None, "chan", "space", None),
        P("space", None),
        P("space", None),
        P("chan", None, None, None),
        P("chan"),
        P("chan", None, None, None),
        P("chan"),
    )
    return jax.shard_map(
        per_device,
        mesh=mesh,
        in_specs=placed,
        out_specs=(P(None, "chan", "space", None), P(None, "chan", "space", None)),
        check_vma=False,
    )
```

```python
import jax
import jax.numpy as jnp
from jax import lax
from jax.sharding import PartitionSpec as P


def shifted(array, axis, by):
    devices = lax.axis_size(axis)
    pairs = [(i, i + by) for i in range(devices) if 0 <= i + by < devices]
    return lax.ppermute(array, axis, pairs)


def remap_window(source, table, first_col, width):
    cycle = table.shape[0]
    cols = (first_col + jnp.arange(width)) % cycle
    picked = lax.dynamic_slice_in_dim(
        jnp.concatenate([table, table], axis=0), first_col % cycle, width, axis=0
    )
    same = source[..., 1 : width + 1]
    prev = source[..., 0:width]
    nxt = source[..., 2 : width + 2]
    zero = jnp.zeros_like(same)
    out = jnp.where(picked == (cols + cycle - 1) % cycle, prev, zero)
    out = jnp.where(picked == (cols + 1) % cycle, nxt, out)
    out = jnp.where(picked == cols, same, out)
    return out


def remap_full(row, table):
    cycle = table.shape[0]
    wrapped = jnp.concatenate([row[..., -1:], row, row[..., :1]], axis=-1)
    return remap_window(wrapped, table, 0, cycle)


def split3(v):
    hi = lax.reduce_precision(v, exponent_bits=8, mantissa_bits=7)
    rest = v - hi
    mid = lax.reduce_precision(rest, exponent_bits=8, mantissa_bits=7)
    lo = rest - mid
    return jnp.stack([hi, mid, lo], -1).astype(jnp.bfloat16)


def join3(parts):
    parts = parts.astype(jnp.float32)
    return (parts[..., 0] + parts[..., 1]) + parts[..., 2]


def conv(x, w, stride):
    return lax.conv_general_dilated(
        x,
        w,
        window_strides=stride,
        padding="VALID",
        dimension_numbers=("NCHW", "OHWI", "NCHW"),
        preferred_element_type=jnp.float32,
    )


def column_windows(padded, groups, halo):
    cycle = padded.shape[-1]
    block = cycle // groups
    lead = padded.shape[:-1]
    left = jnp.roll(padded, halo, axis=-1).reshape(lead + (groups, block))[..., :halo]
    mid = padded.reshape(lead + (groups, block))
    right = jnp.roll(padded, -halo, axis=-1).reshape(lead + (groups, block))[..., block - halo :]
    wins = jnp.concatenate([left, mid, right], axis=-1)
    return jnp.moveaxis(wins, -2, 0)


def pad_to(flat, multiple):
    extra = (-flat.shape[-1]) % multiple
    return jnp.pad(flat, [(0, 0)] * (flat.ndim - 1) + [(0, extra)])


def per_device(features, top_map, bottom_map, first_weight, first_bias, second_weight, second_bias):
    groups = lax.axis_size("chan")
    me = lax.axis_index("chan")
    x = features[0]
    chans = x.shape[0]
    rows = x.shape[1]
    cycle = x.shape[2]
    block = cycle // groups
    upper_map = top_map[0]
    lower_map = bottom_map[0]
    n1 = first_weight.shape[0]
    n2 = second_weight.shape[0]

    halo = 3
    width = block + 2 * halo
    wins = column_windows(x, groups, halo + 1).reshape(groups, -1)
    feat_len = wins.shape[1]

    flat_w = jnp.concatenate(
        [first_weight.reshape(n1, -1), second_weight.reshape(n2, -1)], axis=0
    )
    taps = flat_w.shape[1]
    packed_w = jnp.concatenate(
        [flat_w, split3(jnp.concatenate([first_bias, second_bias]))], axis=1
    ).reshape(1, -1)
    sends = jnp.concatenate([wins, jnp.broadcast_to(packed_w, (groups,) + packed_w.shape[1:])], 1)
    got = lax.all_to_all(pad_to(sends, 1024), "chan", 0, 0, tiled=True)

    tile = got[:, :feat_len].reshape(groups * chans, rows, width + 2)
    every = got[:, feat_len : feat_len + packed_w.shape[1]].reshape(groups, n1 + n2, taps + 3)
    w1 = every[:, :n1, :taps].reshape((-1,) + first_weight.shape[1:])
    w2 = every[:, n1:, :taps].reshape((-1,) + second_weight.shape[1:])
    b1 = join3(every[:, :n1, taps:]).reshape(-1)
    b2 = join3(every[:, n1:, taps:]).reshape(-1)

    prior_lower_map = shifted(lower_map, "space", 1)
    prior = shifted(tile, "space", 1)
    below_src = shifted(tile[:, 0, :], "space", -1)
    start = me * block - halo
    above = remap_window(prior[:, rows - 1, :], upper_map, start, width)
    below = remap_window(below_src, lower_map, start, width)
    prior_below = remap_window(tile[:, 0, :], prior_lower_map, start, width)
    inner = tile[:, :, 1 : width + 1]
    prior_inner = prior[:, :, 1 : width + 1]
    window = jnp.stack(
        [
            jnp.concatenate([above[:, None], inner, below[:, None]], axis=1),
            jnp.concatenate([prior_inner, prior_below[:, None], prior_below[:, None]], axis=1),
        ],
        0,
    )

    pre1 = conv(window, w1, (1, 1))
    both = jax.nn.gelu(pre1 + b1[None, :, None, None]).astype(jnp.bfloat16)
    hidden_win = both[0]
    has_prior = lax.axis_index("space") > 0
    rim_src = jnp.where(has_prior, both[1, :, 0, :], jnp.zeros_like(both[1, :, 0, :]))
    rim = remap_window(rim_src, upper_map, me * block - 1, block + 2)
    stacked = jnp.concatenate([rim[:, None], hidden_win[:, :, 1 : block + 3]], axis=1)
    pre2 = conv(stacked[None], w2, (1, 2))
    coarse_win = jax.nn.gelu(pre2 + b2[None, :, None, None]).astype(jnp.bfloat16)[0]

    hidden_part = hidden_win[:, :, halo - 1 : halo - 1 + block].reshape(groups, -1)
    coarse_part = coarse_win.reshape(groups, -1)
    back = lax.all_to_all(
        jnp.concatenate([hidden_part, coarse_part], 1), "chan", 0, 0, tiled=True
    )
    h_len = hidden_part.shape[1]
    hidden_out = back[:, :h_len].reshape((groups, chans, rows, block))
    hidden_out = jnp.moveaxis(hidden_out, 0, 2).reshape(chans, rows, cycle)
    coarse_shape = coarse_win.shape
    coarse_out = back[:, h_len:].reshape(
        (groups, coarse_shape[0] // groups) + coarse_shape[1:]
    )
    coarse_out = jnp.moveaxis(coarse_out, 0, 2).reshape(
        (coarse_shape[0] // groups, coarse_shape[1], groups * coarse_shape[2])
    )
    return hidden_out[None], coarse_out[None]


def solution(mesh):
    placed = (
        P(None, "chan", "space", None),
        P("space", None),
        P("space", None),
        P("chan", None, None, None),
        P("chan"),
        P("chan", None, None, None),
        P("chan"),
    )
    return jax.shard_map(
        per_device,
        mesh=mesh,
        in_specs=placed,
        out_specs=(P(None, "chan", "space", None), P(None, "chan", "space", None)),
        check_vma=False,
    )
```

```python
import jax
import jax.numpy as jnp
from jax import lax
from jax.sharding import PartitionSpec as P


def shifted(array, axis, by):
    devices = lax.axis_size(axis)
    pairs = [(i, i + by) for i in range(devices) if 0 <= i + by < devices]
    return lax.ppermute(array, axis, pairs)


def remap_window(source, table, first_col, width):
    cycle = table.shape[0]
    cols = (first_col + jnp.arange(width)) % cycle
    picked = lax.dynamic_slice_in_dim(
        jnp.concatenate([table, table], axis=0), first_col % cycle, width, axis=0
    )
    same = source[..., 1 : width + 1]
    prev = source[..., 0:width]
    nxt = source[..., 2 : width + 2]
    zero = jnp.zeros_like(same)
    out = jnp.where(picked == (cols + cycle - 1) % cycle, prev, zero)
    out = jnp.where(picked == (cols + 1) % cycle, nxt, out)
    out = jnp.where(picked == cols, same, out)
    return out


def remap_full(row, table):
    cycle = table.shape[0]
    wrapped = jnp.concatenate([row[..., -1:], row, row[..., :1]], axis=-1)
    return remap_window(wrapped, table, 0, cycle)


def split3(v):
    hi = lax.reduce_precision(v, exponent_bits=8, mantissa_bits=7)
    rest = v - hi
    mid = lax.reduce_precision(rest, exponent_bits=8, mantissa_bits=7)
    lo = rest - mid
    return jnp.stack([hi, mid, lo], -1).astype(jnp.bfloat16)


def join3(parts):
    parts = parts.astype(jnp.float32)
    return (parts[..., 0] + parts[..., 1]) + parts[..., 2]


def conv(x, w, stride):
    return lax.conv_general_dilated(
        x,
        w,
        window_strides=stride,
        padding="VALID",
        dimension_numbers=("NCHW", "OHWI", "NCHW"),
        preferred_element_type=jnp.float32,
    )


def column_windows(padded, groups, halo):
    cycle = padded.shape[-1]
    block = cycle // groups
    lead = padded.shape[:-1]
    left = jnp.roll(padded, halo, axis=-1).reshape(lead + (groups, block))[..., :halo]
    mid = padded.reshape(lead + (groups, block))
    right = jnp.roll(padded, -halo, axis=-1).reshape(lead + (groups, block))[..., block - halo :]
    wins = jnp.concatenate([left, mid, right], axis=-1)
    return jnp.moveaxis(wins, -2, 0)


def gather_space(part):
    count = lax.axis_size("space")
    me = lax.axis_index("space")
    acc = part[None]
    bit = count // 2
    while bit >= 1:
        recv = lax.ppermute(acc, "space", [(i, i ^ bit) for i in range(count)])
        low = (me & bit) == 0
        pair = jnp.where(low, jnp.stack([acc, recv], 1), jnp.stack([recv, acc], 1))
        acc = pair.reshape((-1,) + part.shape)
        bit //= 2
    return acc


def pad_to(flat, multiple):
    extra = (-flat.shape[-1]) % multiple
    return jnp.pad(flat, [(0, 0)] * (flat.ndim - 1) + [(0, extra)])


def per_device(features, top_map, bottom_map, first_weight, first_bias, second_weight, second_bias):
    groups = lax.axis_size("chan")
    me = lax.axis_index("chan")
    x = features[0]
    chans = x.shape[0]
    rows = x.shape[1]
    cycle = x.shape[2]
    block = cycle // groups
    upper_map = top_map[0]
    lower_map = bottom_map[0]
    n1 = first_weight.shape[0]
    n2 = second_weight.shape[0]

    halo = 3
    width = block + 2 * halo
    wins = column_windows(x, groups, halo + 1).reshape(groups, -1)
    feat_len = wins.shape[1]

    flat_w = jnp.concatenate(
        [first_weight.reshape(n1, -1), second_weight.reshape(n2, -1)], axis=0
    )
    taps = flat_w.shape[1]
    packed_w = jnp.concatenate(
        [flat_w, split3(jnp.concatenate([first_bias, second_bias]))], axis=1
    ).reshape(-1)
    tiles = lax.axis_size("space")
    piece = -(-packed_w.shape[0] // (tiles * 128)) * 128
    packed_w = jnp.pad(packed_w, (0, piece * tiles - packed_w.shape[0]))
    my_piece = lax.dynamic_slice_in_dim(packed_w, lax.axis_index("space") * piece, piece)
    sends = jnp.concatenate([wins, jnp.broadcast_to(my_piece[None], (groups, piece))], 1)
    got = lax.all_to_all(pad_to(sends, 1024), "chan", 0, 0, tiled=True)

    tile = got[:, :feat_len].reshape(groups * chans, rows, width + 2)
    pieces = gather_space(got[:, feat_len : feat_len + piece])
    every = jnp.moveaxis(pieces, 0, 1).reshape(groups, -1)
    every = every[:, : (n1 + n2) * (taps + 3)].reshape(groups, n1 + n2, taps + 3)
    w1 = every[:, :n1, :taps].reshape((-1,) + first_weight.shape[1:])
    w2 = every[:, n1:, :taps].reshape((-1,) + second_weight.shape[1:])
    b1 = join3(every[:, :n1, taps:]).reshape(-1)
    b2 = join3(every[:, n1:, taps:]).reshape(-1)

    prior_lower_map = shifted(lower_map, "space", 1)
    prior = shifted(tile, "space", 1)
    below_src = shifted(tile[:, 0, :], "space", -1)
    start = me * block - halo
    above = remap_window(prior[:, rows - 1, :], upper_map, start, width)
    below = remap_window(below_src, lower_map, start, width)
    prior_below = remap_window(tile[:, 0, :], prior_lower_map, start, width)
    inner = tile[:, :, 1 : width + 1]
    prior_inner = prior[:, :, 1 : width + 1]
    window = jnp.stack(
        [
            jnp.concatenate([above[:, None], inner, below[:, None]], axis=1),
            jnp.concatenate([prior_inner, prior_below[:, None], prior_below[:, None]], axis=1),
        ],
        0,
    )

    pre1 = conv(window, w1, (1, 1))
    both = jax.nn.gelu(pre1 + b1[None, :, None, None]).astype(jnp.bfloat16)
    hidden_win = both[0]
    has_prior = lax.axis_index("space") > 0
    rim_src = jnp.where(has_prior, both[1, :, 0, :], jnp.zeros_like(both[1, :, 0, :]))
    rim = remap_window(rim_src, upper_map, me * block - 1, block + 2)
    stacked = jnp.concatenate([rim[:, None], hidden_win[:, :, 1 : block + 3]], axis=1)
    pre2 = conv(stacked[None], w2, (1, 2))
    coarse_win = jax.nn.gelu(pre2 + b2[None, :, None, None]).astype(jnp.bfloat16)[0]

    hidden_part = hidden_win[:, :, halo - 1 : halo - 1 + block].reshape(groups, -1)
    coarse_part = coarse_win.reshape(groups, -1)
    back = lax.all_to_all(
        jnp.concatenate([hidden_part, coarse_part], 1), "chan", 0, 0, tiled=True
    )
    h_len = hidden_part.shape[1]
    hidden_out = back[:, :h_len].reshape((groups, chans, rows, block))
    hidden_out = jnp.moveaxis(hidden_out, 0, 2).reshape(chans, rows, cycle)
    coarse_shape = coarse_win.shape
    coarse_out = back[:, h_len:].reshape(
        (groups, coarse_shape[0] // groups) + coarse_shape[1:]
    )
    coarse_out = jnp.moveaxis(coarse_out, 0, 2).reshape(
        (coarse_shape[0] // groups, coarse_shape[1], groups * coarse_shape[2])
    )
    return hidden_out[None], coarse_out[None]


def solution(mesh):
    placed = (
        P(None, "chan", "space", None),
        P("space", None),
        P("space", None),
        P("chan", None, None, None),
        P("chan"),
        P("chan", None, None, None),
        P("chan"),
    )
    return jax.shard_map(
        per_device,
        mesh=mesh,
        in_specs=placed,
        out_specs=(P(None, "chan", "space", None), P(None, "chan", "space", None)),
        check_vma=False,
    )
```

```python
import jax
import jax.numpy as jnp
from jax import lax
from jax.sharding import PartitionSpec as P


def shifted(array, axis, by):
    devices = lax.axis_size(axis)
    pairs = [(i, i + by) for i in range(devices) if 0 <= i + by < devices]
    return lax.ppermute(array, axis, pairs)


def remap_window(source, table, first_col, width):
    cycle = table.shape[0]
    cols = (first_col + jnp.arange(width)) % cycle
    picked = lax.dynamic_slice_in_dim(
        jnp.concatenate([table, table], axis=0), first_col % cycle, width, axis=0
    )
    same = source[..., 1 : width + 1]
    prev = source[..., 0:width]
    nxt = source[..., 2 : width + 2]
    zero = jnp.zeros_like(same)
    out = jnp.where(picked == (cols + cycle - 1) % cycle, prev, zero)
    out = jnp.where(picked == (cols + 1) % cycle, nxt, out)
    out = jnp.where(picked == cols, same, out)
    return out


def remap_full(row, table):
    cycle = table.shape[0]
    wrapped = jnp.concatenate([row[..., -1:], row, row[..., :1]], axis=-1)
    return remap_window(wrapped, table, 0, cycle)


def split3(v):
    hi = lax.reduce_precision(v, exponent_bits=8, mantissa_bits=7)
    rest = v - hi
    mid = lax.reduce_precision(rest, exponent_bits=8, mantissa_bits=7)
    lo = rest - mid
    return jnp.stack([hi, mid, lo], -1).astype(jnp.bfloat16)


def join3(parts):
    parts = parts.astype(jnp.float32)
    return (parts[..., 0] + parts[..., 1]) + parts[..., 2]


def conv(x, w, stride):
    return lax.conv_general_dilated(
        x,
        w,
        window_strides=stride,
        padding="VALID",
        dimension_numbers=("NCHW", "OHWI", "NCHW"),
        preferred_element_type=jnp.float32,
    )


def column_windows(padded, groups, halo):
    cycle = padded.shape[-1]
    block = cycle // groups
    lead = padded.shape[:-1]
    left = jnp.roll(padded, halo, axis=-1).reshape(lead + (groups, block))[..., :halo]
    mid = padded.reshape(lead + (groups, block))
    right = jnp.roll(padded, -halo, axis=-1).reshape(lead + (groups, block))[..., block - halo :]
    wins = jnp.concatenate([left, mid, right], axis=-1)
    return jnp.moveaxis(wins, -2, 0)


def pad_to(flat, multiple):
    extra = (-flat.shape[-1]) % multiple
    return jnp.pad(flat, [(0, 0)] * (flat.ndim - 1) + [(0, extra)])


def per_device(features, top_map, bottom_map, first_weight, first_bias, second_weight, second_bias):
    groups = lax.axis_size("chan")
    me = lax.axis_index("chan")
    x = features[0]
    chans = x.shape[0]
    rows = x.shape[1]
    cycle = x.shape[2]
    block = cycle // groups
    upper_map = top_map[0]
    lower_map = bottom_map[0]
    n1 = first_weight.shape[0]
    n2 = second_weight.shape[0]

    halo = 3
    width = block + 2 * halo
    wins = column_windows(x, groups, halo + 1).reshape(groups, -1)
    feat_len = wins.shape[1]

    flat_w = jnp.concatenate(
        [first_weight.reshape(n1, -1), second_weight.reshape(n2, -1)], axis=0
    )
    taps = flat_w.shape[1]
    packed_w = jnp.concatenate(
        [flat_w, split3(jnp.concatenate([first_bias, second_bias]))], axis=1
    ).reshape(1, -1)
    w_got = lax.all_to_all(
        pad_to(jnp.broadcast_to(packed_w, (groups,) + packed_w.shape[1:]), 1024),
        "chan", 0, 0, tiled=True,
    )
    got = lax.all_to_all(pad_to(wins, 1024), "chan", 0, 0, tiled=True)

    tile = got[:, :feat_len].reshape(groups * chans, rows, width + 2)
    every = w_got[:, : packed_w.shape[1]].reshape(groups, n1 + n2, taps + 3)
    w1 = every[:, :n1, :taps].reshape((-1,) + first_weight.shape[1:])
    w2 = every[:, n1:, :taps].reshape((-1,) + second_weight.shape[1:])
    b1 = join3(every[:, :n1, taps:]).reshape(-1)
    b2 = join3(every[:, n1:, taps:]).reshape(-1)

    prior_lower_map = shifted(lower_map, "space", 1)
    prior = shifted(tile, "space", 1)
    below_src = shifted(tile[:, 0, :], "space", -1)
    start = me * block - halo
    above = remap_window(prior[:, rows - 1, :], upper_map, start, width)
    below = remap_window(below_src, lower_map, start, width)
    prior_below = remap_window(tile[:, 0, :], prior_lower_map, start, width)
    inner = tile[:, :, 1 : width + 1]
    prior_inner = prior[:, :, 1 : width + 1]
    window = jnp.stack(
        [
            jnp.concatenate([above[:, None], inner, below[:, None]], axis=1),
            jnp.concatenate([prior_inner, prior_below[:, None], prior_below[:, None]], axis=1),
        ],
        0,
    )

    pre1 = conv(window, w1, (1, 1))
    both = jax.nn.gelu(pre1 + b1[None, :, None, None]).astype(jnp.bfloat16)
    hidden_win = both[0]
    has_prior = lax.axis_index("space") > 0
    rim_src = jnp.where(has_prior, both[1, :, 0, :], jnp.zeros_like(both[1, :, 0, :]))
    rim = remap_window(rim_src, upper_map, me * block - 1, block + 2)
    stacked = jnp.concatenate([rim[:, None], hidden_win[:, :, 1 : block + 3]], axis=1)
    pre2 = conv(stacked[None], w2, (1, 2))
    coarse_win = jax.nn.gelu(pre2 + b2[None, :, None, None]).astype(jnp.bfloat16)[0]

    hidden_part = hidden_win[:, :, halo - 1 : halo - 1 + block].reshape(groups, -1)
    coarse_part = coarse_win.reshape(groups, -1)
    back = lax.all_to_all(
        jnp.concatenate([hidden_part, coarse_part], 1), "chan", 0, 0, tiled=True
    )
    h_len = hidden_part.shape[1]
    hidden_out = back[:, :h_len].reshape((groups, chans, rows, block))
    hidden_out = jnp.moveaxis(hidden_out, 0, 2).reshape(chans, rows, cycle)
    coarse_shape = coarse_win.shape
    coarse_out = back[:, h_len:].reshape(
        (groups, coarse_shape[0] // groups) + coarse_shape[1:]
    )
    coarse_out = jnp.moveaxis(coarse_out, 0, 2).reshape(
        (coarse_shape[0] // groups, coarse_shape[1], groups * coarse_shape[2])
    )
    return hidden_out[None], coarse_out[None]


def solution(mesh):
    placed = (
        P(None, "chan", "space", None),
        P("space", None),
        P("space", None),
        P("chan", None, None, None),
        P("chan"),
        P("chan", None, None, None),
        P("chan"),
    )
    return jax.shard_map(
        per_device,
        mesh=mesh,
        in_specs=placed,
        out_specs=(P(None, "chan", "space", None), P(None, "chan", "space", None)),
        check_vma=False,
    )
```

```python
import jax
import jax.numpy as jnp
from jax import lax
from jax.sharding import PartitionSpec as P


def shifted(array, axis, by):
    devices = lax.axis_size(axis)
    pairs = [(i, i + by) for i in range(devices) if 0 <= i + by < devices]
    return lax.ppermute(array, axis, pairs)


def remap_window(source, table, first_col, width):
    cycle = table.shape[0]
    cols = (first_col + jnp.arange(width)) % cycle
    picked = lax.dynamic_slice_in_dim(
        jnp.concatenate([table, table], axis=0), first_col % cycle, width, axis=0
    )
    same = source[..., 1 : width + 1]
    prev = source[..., 0:width]
    nxt = source[..., 2 : width + 2]
    zero = jnp.zeros_like(same)
    out = jnp.where(picked == (cols + cycle - 1) % cycle, prev, zero)
    out = jnp.where(picked == (cols + 1) % cycle, nxt, out)
    out = jnp.where(picked == cols, same, out)
    return out


def remap_full(row, table):
    cycle = table.shape[0]
    wrapped = jnp.concatenate([row[..., -1:], row, row[..., :1]], axis=-1)
    return remap_window(wrapped, table, 0, cycle)


def split3(v):
    hi = lax.reduce_precision(v, exponent_bits=8, mantissa_bits=7)
    rest = v - hi
    mid = lax.reduce_precision(rest, exponent_bits=8, mantissa_bits=7)
    lo = rest - mid
    return jnp.stack([hi, mid, lo], -1).astype(jnp.bfloat16)


def join3(parts):
    parts = parts.astype(jnp.float32)
    return (parts[..., 0] + parts[..., 1]) + parts[..., 2]


def conv(x, w, stride):
    return lax.conv_general_dilated(
        x,
        w,
        window_strides=stride,
        padding="VALID",
        dimension_numbers=("NCHW", "OHWI", "NCHW"),
        preferred_element_type=jnp.float32,
    )


def column_windows(padded, groups, halo):
    cycle = padded.shape[-1]
    block = cycle // groups
    lead = padded.shape[:-1]
    left = jnp.roll(padded, halo, axis=-1).reshape(lead + (groups, block))[..., :halo]
    mid = padded.reshape(lead + (groups, block))
    right = jnp.roll(padded, -halo, axis=-1).reshape(lead + (groups, block))[..., block - halo :]
    wins = jnp.concatenate([left, mid, right], axis=-1)
    return jnp.moveaxis(wins, -2, 0)


def pad_to(flat, multiple):
    extra = (-flat.shape[-1]) % multiple
    return jnp.pad(flat, [(0, 0)] * (flat.ndim - 1) + [(0, extra)])


def per_device(features, top_map, bottom_map, first_weight, first_bias, second_weight, second_bias):
    groups = lax.axis_size("chan")
    me = lax.axis_index("chan")
    x = features[0]
    chans = x.shape[0]
    rows = x.shape[1]
    cycle = x.shape[2]
    block = cycle // groups
    upper_map = top_map[0]
    lower_map = bottom_map[0]
    n1 = first_weight.shape[0]
    n2 = second_weight.shape[0]

    halo = 3
    width = block + 2 * halo
    wins = column_windows(x, groups, halo + 1).reshape(groups, -1)
    feat_len = wins.shape[1]

    flat_w = jnp.concatenate(
        [first_weight.reshape(n1, -1), second_weight.reshape(n2, -1)], axis=0
    )
    taps = flat_w.shape[1]
    packed_w = jnp.concatenate(
        [flat_w, split3(jnp.concatenate([first_bias, second_bias]))], axis=1
    ).reshape(-1)
    w_len = packed_w.shape[0]
    half = -(-w_len // 256) * 128
    packed_w = jnp.pad(packed_w, (0, 2 * half - w_len))
    second = (lax.axis_index("space") % 2) == 1
    mine = lax.dynamic_slice_in_dim(packed_w, jnp.where(second, half, 0), half)
    sends = jnp.concatenate([wins, jnp.broadcast_to(mine[None], (groups, half))], 1)
    got = lax.all_to_all(pad_to(sends, 1024), "chan", 0, 0, tiled=True)

    tile = got[:, :feat_len].reshape(groups * chans, rows, width + 2)
    own_half = got[:, feat_len : feat_len + half]
    spaces = lax.axis_size("space")
    other_half = lax.ppermute(own_half, "space", [(i, i ^ 1) for i in range(spaces)])
    every = jnp.where(
        second,
        jnp.concatenate([other_half, own_half], 1),
        jnp.concatenate([own_half, other_half], 1),
    )
    every = every[:, :w_len].reshape(groups, n1 + n2, taps + 3)
    w1 = every[:, :n1, :taps].reshape((-1,) + first_weight.shape[1:])
    w2 = every[:, n1:, :taps].reshape((-1,) + second_weight.shape[1:])
    b1 = join3(every[:, :n1, taps:]).reshape(-1)
    b2 = join3(every[:, n1:, taps:]).reshape(-1)

    prior_lower_map = shifted(lower_map, "space", 1)
    prior = shifted(tile, "space", 1)
    below_src = shifted(tile[:, 0, :], "space", -1)
    start = me * block - halo
    above = remap_window(prior[:, rows - 1, :], upper_map, start, width)
    below = remap_window(below_src, lower_map, start, width)
    prior_below = remap_window(tile[:, 0, :], prior_lower_map, start, width)
    inner = tile[:, :, 1 : width + 1]
    prior_inner = prior[:, :, 1 : width + 1]
    window = jnp.stack(
        [
            jnp.concatenate([above[:, None], inner, below[:, None]], axis=1),
            jnp.concatenate([prior_inner, prior_below[:, None], prior_below[:, None]], axis=1),
        ],
        0,
    )

    pre1 = conv(window, w1, (1, 1))
    both = jax.nn.gelu(pre1 + b1[None, :, None, None]).astype(jnp.bfloat16)
    hidden_win = both[0]
    has_prior = lax.axis_index("space") > 0
    rim_src = jnp.where(has_prior, both[1, :, 0, :], jnp.zeros_like(both[1, :, 0, :]))
    rim = remap_window(rim_src, upper_map, me * block - 1, block + 2)
    stacked = jnp.concatenate([rim[:, None], hidden_win[:, :, 1 : block + 3]], axis=1)
    pre2 = conv(stacked[None], w2, (1, 2))
    coarse_win = jax.nn.gelu(pre2 + b2[None, :, None, None]).astype(jnp.bfloat16)[0]

    hidden_part = hidden_win[:, :, halo - 1 : halo - 1 + block].reshape(groups, -1)
    coarse_part = coarse_win.reshape(groups, -1)
    back = lax.all_to_all(
        jnp.concatenate([hidden_part, coarse_part], 1), "chan", 0, 0, tiled=True
    )
    h_len = hidden_part.shape[1]
    hidden_out = back[:, :h_len].reshape((groups, chans, rows, block))
    hidden_out = jnp.moveaxis(hidden_out, 0, 2).reshape(chans, rows, cycle)
    coarse_shape = coarse_win.shape
    coarse_out = back[:, h_len:].reshape(
        (groups, coarse_shape[0] // groups) + coarse_shape[1:]
    )
    coarse_out = jnp.moveaxis(coarse_out, 0, 2).reshape(
        (coarse_shape[0] // groups, coarse_shape[1], groups * coarse_shape[2])
    )
    return hidden_out[None], coarse_out[None]


def solution(mesh):
    placed = (
        P(None, "chan", "space", None),
        P("space", None),
        P("space", None),
        P("chan", None, None, None),
        P("chan"),
        P("chan", None, None, None),
        P("chan"),
    )
    return jax.shard_map(
        per_device,
        mesh=mesh,
        in_specs=placed,
        out_specs=(P(None, "chan", "space", None), P(None, "chan", "space", None)),
        check_vma=False,
    )
```

```python
import jax
import jax.numpy as jnp
from jax import lax
from jax.sharding import PartitionSpec as P


def shifted(array, axis, by):
    devices = lax.axis_size(axis)
    pairs = [(i, i + by) for i in range(devices) if 0 <= i + by < devices]
    return lax.ppermute(array, axis, pairs)


def remap_window(source, table, first_col, width):
    cycle = table.shape[0]
    cols = (first_col + jnp.arange(width)) % cycle
    picked = lax.dynamic_slice_in_dim(
        jnp.concatenate([table, table], axis=0), first_col % cycle, width, axis=0
    )
    same = source[..., 1 : width + 1]
    prev = source[..., 0:width]
    nxt = source[..., 2 : width + 2]
    zero = jnp.zeros_like(same)
    out = jnp.where(picked == (cols + cycle - 1) % cycle, prev, zero)
    out = jnp.where(picked == (cols + 1) % cycle, nxt, out)
    out = jnp.where(picked == cols, same, out)
    return out


def remap_full(row, table):
    cycle = table.shape[0]
    wrapped = jnp.concatenate([row[..., -1:], row, row[..., :1]], axis=-1)
    return remap_window(wrapped, table, 0, cycle)


def split3(v):
    hi = lax.reduce_precision(v, exponent_bits=8, mantissa_bits=7)
    rest = v - hi
    mid = lax.reduce_precision(rest, exponent_bits=8, mantissa_bits=7)
    lo = rest - mid
    return jnp.stack([hi, mid, lo], -1).astype(jnp.bfloat16)


def join3(parts):
    parts = parts.astype(jnp.float32)
    return (parts[..., 0] + parts[..., 1]) + parts[..., 2]


def conv(x, w, stride):
    return lax.conv_general_dilated(
        x,
        w,
        window_strides=stride,
        padding="VALID",
        dimension_numbers=("NCHW", "OHWI", "NCHW"),
        preferred_element_type=jnp.float32,
    )


def column_windows(padded, groups, halo):
    cycle = padded.shape[-1]
    block = cycle // groups
    lead = padded.shape[:-1]
    left = jnp.roll(padded, halo, axis=-1).reshape(lead + (groups, block))[..., :halo]
    mid = padded.reshape(lead + (groups, block))
    right = jnp.roll(padded, -halo, axis=-1).reshape(lead + (groups, block))[..., block - halo :]
    wins = jnp.concatenate([left, mid, right], axis=-1)
    return jnp.moveaxis(wins, -2, 0)


def pad_to(flat, multiple):
    extra = (-flat.shape[-1]) % multiple
    return jnp.pad(flat, [(0, 0)] * (flat.ndim - 1) + [(0, extra)])


def per_device(features, top_map, bottom_map, first_weight, first_bias, second_weight, second_bias):
    groups = lax.axis_size("chan")
    me = lax.axis_index("chan")
    x = features[0]
    chans = x.shape[0]
    rows = x.shape[1]
    cycle = x.shape[2]
    block = cycle // groups
    upper_map = top_map[0]
    lower_map = bottom_map[0]
    n1 = first_weight.shape[0]
    n2 = second_weight.shape[0]

    halo = 3
    width = block + 2 * halo
    wins = column_windows(x, groups, halo + 1).reshape(groups, -1)
    feat_len = wins.shape[1]

    flat_w = jnp.concatenate(
        [first_weight.reshape(n1, -1), second_weight.reshape(n2, -1)], axis=0
    )
    taps = flat_w.shape[1]
    packed_w = jnp.concatenate(
        [flat_w.reshape(-1), split3(jnp.concatenate([first_bias, second_bias])).reshape(-1)]
    )
    w_len = packed_w.shape[0]
    half = -(-w_len // 256) * 128
    packed_w = jnp.pad(packed_w, (0, 2 * half - w_len))
    second = (lax.axis_index("space") % 2) == 1
    mine = lax.dynamic_slice_in_dim(packed_w, jnp.where(second, half, 0), half)
    sends = jnp.concatenate([wins, jnp.broadcast_to(mine[None], (groups, half))], 1)
    got = lax.all_to_all(
        pad_to(sends, 256).reshape(groups, 2, -1), "chan", 0, 0, tiled=True
    ).reshape(groups, -1)

    tile = got[:, :feat_len].reshape(groups * chans, rows, width + 2)
    own_half = got[:, feat_len : feat_len + half]
    spaces = lax.axis_size("space")
    other_half = lax.ppermute(own_half, "space", [(i, i ^ 1) for i in range(spaces)])
    every = jnp.where(
        second,
        jnp.concatenate([other_half, own_half], 1),
        jnp.concatenate([own_half, other_half], 1),
    )
    w_all = every[:, : (n1 + n2) * taps].reshape(groups, n1 + n2, taps)
    b_all = every[:, (n1 + n2) * taps : w_len].reshape(groups, n1 + n2, 3)
    w1 = w_all[:, :n1].reshape((-1,) + first_weight.shape[1:])
    w2 = w_all[:, n1:].reshape((-1,) + second_weight.shape[1:])
    b1 = join3(b_all[:, :n1]).reshape(-1)
    b2 = join3(b_all[:, n1:]).reshape(-1)

    prior_lower_map = shifted(lower_map, "space", 1)
    prior = shifted(tile, "space", 1)
    below_src = shifted(tile[:, 0, :], "space", -1)
    start = me * block - halo
    above = remap_window(prior[:, rows - 1, :], upper_map, start, width)
    below = remap_window(below_src, lower_map, start, width)
    prior_below = remap_window(tile[:, 0, :], prior_lower_map, start, width)
    inner = tile[:, :, 1 : width + 1]
    prior_inner = prior[:, :, 1 : width + 1]
    window = jnp.stack(
        [
            jnp.concatenate([above[:, None], inner, below[:, None]], axis=1),
            jnp.concatenate([prior_inner, prior_below[:, None], prior_below[:, None]], axis=1),
        ],
        0,
    )

    pre1 = conv(window, w1, (1, 1))
    both = jax.nn.gelu(pre1 + b1[None, :, None, None]).astype(jnp.bfloat16)
    hidden_win = both[0]
    has_prior = lax.axis_index("space") > 0
    rim_src = jnp.where(has_prior, both[1, :, 0, :], jnp.zeros_like(both[1, :, 0, :]))
    rim = remap_window(rim_src, upper_map, me * block - 1, block + 2)
    stacked = jnp.concatenate([rim[:, None], hidden_win[:, :, 1 : block + 3]], axis=1)
    pre2 = conv(stacked[None], w2, (1, 2))
    coarse_win = jax.nn.gelu(pre2 + b2[None, :, None, None]).astype(jnp.bfloat16)[0]

    hidden_part = hidden_win[:, :, halo - 1 : halo - 1 + block].reshape(groups, -1)
    coarse_part = coarse_win.reshape(groups, -1)
    back = lax.all_to_all(
        jnp.concatenate([hidden_part, coarse_part], 1).reshape(groups, 2, -1),
        "chan", 0, 0, tiled=True,
    ).reshape(groups, -1)
    h_len = hidden_part.shape[1]
    hidden_out = back[:, :h_len].reshape((groups, chans, rows, block))
    hidden_out = jnp.moveaxis(hidden_out, 0, 2).reshape(chans, rows, cycle)
    coarse_shape = coarse_win.shape
    coarse_out = back[:, h_len:].reshape(
        (groups, coarse_shape[0] // groups) + coarse_shape[1:]
    )
    coarse_out = jnp.moveaxis(coarse_out, 0, 2).reshape(
        (coarse_shape[0] // groups, coarse_shape[1], groups * coarse_shape[2])
    )
    return hidden_out[None], coarse_out[None]


def solution(mesh):
    placed = (
        P(None, "chan", "space", None),
        P("space", None),
        P("space", None),
        P("chan", None, None, None),
        P("chan"),
        P("chan", None, None, None),
        P("chan"),
    )
    return jax.shard_map(
        per_device,
        mesh=mesh,
        in_specs=placed,
        out_specs=(P(None, "chan", "space", None), P(None, "chan", "space", None)),
        check_vma=False,
    )
```

```python
import jax
import jax.numpy as jnp
from jax import lax
from jax.sharding import PartitionSpec as P


def shifted(array, axis, by):
    devices = lax.axis_size(axis)
    pairs = [(i, i + by) for i in range(devices) if 0 <= i + by < devices]
    return lax.ppermute(array, axis, pairs)


def rim_code(table, first_col, width):
    cycle = table.shape[0]
    cols = (first_col + jnp.arange(width)) % cycle
    picked = lax.dynamic_slice_in_dim(
        jnp.concatenate([table, table], axis=0), first_col % cycle, width, axis=0
    )
    code = jnp.where(picked == (cols + cycle - 1) % cycle, -1, 2)
    code = jnp.where(picked == (cols + 1) % cycle, 1, code)
    code = jnp.where(picked == cols, 0, code)
    return code.astype(jnp.bfloat16)


def apply_code(source, code):
    width = code.shape[0]
    same = source[..., 1 : width + 1]
    prev = source[..., 0:width]
    nxt = source[..., 2 : width + 2]
    zero = jnp.zeros_like(same)
    out = jnp.where(code == -1, prev, zero)
    out = jnp.where(code == 1, nxt, out)
    out = jnp.where(code == 0, same, out)
    return out


def remap_window(source, table, first_col, width):
    return apply_code(source, rim_code(table, first_col, width))


def remap_full(row, table):
    cycle = table.shape[0]
    wrapped = jnp.concatenate([row[..., -1:], row, row[..., :1]], axis=-1)
    return remap_window(wrapped, table, 0, cycle)


def split3(v):
    hi = lax.reduce_precision(v, exponent_bits=8, mantissa_bits=7)
    rest = v - hi
    mid = lax.reduce_precision(rest, exponent_bits=8, mantissa_bits=7)
    lo = rest - mid
    return jnp.stack([hi, mid, lo], -1).astype(jnp.bfloat16)


def join3(parts):
    parts = parts.astype(jnp.float32)
    return (parts[..., 0] + parts[..., 1]) + parts[..., 2]


def conv(x, w, stride):
    return lax.conv_general_dilated(
        x,
        w,
        window_strides=stride,
        padding="VALID",
        dimension_numbers=("NCHW", "OHWI", "NCHW"),
        preferred_element_type=jnp.float32,
    )


def column_windows(padded, groups, halo):
    cycle = padded.shape[-1]
    block = cycle // groups
    lead = padded.shape[:-1]
    left = jnp.roll(padded, halo, axis=-1).reshape(lead + (groups, block))[..., :halo]
    mid = padded.reshape(lead + (groups, block))
    right = jnp.roll(padded, -halo, axis=-1).reshape(lead + (groups, block))[..., block - halo :]
    wins = jnp.concatenate([left, mid, right], axis=-1)
    return jnp.moveaxis(wins, -2, 0)


def pad_to(flat, multiple):
    extra = (-flat.shape[-1]) % multiple
    return jnp.pad(flat, [(0, 0)] * (flat.ndim - 1) + [(0, extra)])


def per_device(features, top_map, bottom_map, first_weight, first_bias, second_weight, second_bias):
    groups = lax.axis_size("chan")
    me = lax.axis_index("chan")
    x = features[0]
    chans = x.shape[0]
    rows = x.shape[1]
    cycle = x.shape[2]
    block = cycle // groups
    upper_map = top_map[0]
    lower_map = bottom_map[0]
    n1 = first_weight.shape[0]
    n2 = second_weight.shape[0]

    halo = 3
    width = block + 2 * halo
    wins = column_windows(x, groups, halo + 1).reshape(groups, -1)
    feat_len = wins.shape[1]

    flat_w = jnp.concatenate(
        [first_weight.reshape(n1, -1), second_weight.reshape(n2, -1)], axis=0
    )
    taps = flat_w.shape[1]
    packed_w = jnp.concatenate(
        [flat_w.reshape(-1), split3(jnp.concatenate([first_bias, second_bias])).reshape(-1)]
    )
    w_len = packed_w.shape[0]
    half = -(-w_len // 256) * 128
    packed_w = jnp.pad(packed_w, (0, 2 * half - w_len))
    second = (lax.axis_index("space") % 2) == 1
    mine = lax.dynamic_slice_in_dim(packed_w, jnp.where(second, half, 0), half)
    sends = jnp.concatenate([wins, jnp.broadcast_to(mine[None], (groups, half))], 1)
    got = lax.all_to_all(
        pad_to(sends, 256).reshape(groups, 2, -1), "chan", 0, 0, tiled=True
    ).reshape(groups, -1)

    tile = got[:, :feat_len].reshape(groups * chans, rows, width + 2)
    own_half = got[:, feat_len : feat_len + half]
    spaces = lax.axis_size("space")
    other_half = lax.ppermute(own_half, "space", [(i, i ^ 1) for i in range(spaces)])
    every = jnp.where(
        second,
        jnp.concatenate([other_half, own_half], 1),
        jnp.concatenate([own_half, other_half], 1),
    )
    w_all = every[:, : (n1 + n2) * taps].reshape(groups, n1 + n2, taps)
    b_all = every[:, (n1 + n2) * taps : w_len].reshape(groups, n1 + n2, 3)
    w1 = w_all[:, :n1].reshape((-1,) + first_weight.shape[1:])
    w2 = w_all[:, n1:].reshape((-1,) + second_weight.shape[1:])
    b1 = join3(b_all[:, :n1]).reshape(-1)
    b2 = join3(b_all[:, n1:]).reshape(-1)

    start = me * block - halo
    lower_code = rim_code(lower_map, start, width)
    code_rows = jnp.broadcast_to(jnp.pad(lower_code, (1, 1))[None, None], (1, rows, width + 2))
    prior_ext = shifted(jnp.concatenate([tile, code_rows], 0), "space", 1)
    prior = prior_ext[: groups * chans]
    prior_code = prior_ext[groups * chans, 0, 1 : width + 1]
    below_src = shifted(tile[:, 0, :], "space", -1)
    above = remap_window(prior[:, rows - 1, :], upper_map, start, width)
    below = apply_code(below_src, lower_code)
    prior_below = apply_code(tile[:, 0, :], prior_code)
    inner = tile[:, :, 1 : width + 1]
    prior_inner = prior[:, :, 1 : width + 1]
    window = jnp.stack(
        [
            jnp.concatenate([above[:, None], inner, below[:, None]], axis=1),
            jnp.concatenate([prior_inner, prior_below[:, None], prior_below[:, None]], axis=1),
        ],
        0,
    )

    pre1 = conv(window, w1, (1, 1))
    both = jax.nn.gelu(pre1 + b1[None, :, None, None]).astype(jnp.bfloat16)
    hidden_win = both[0]
    has_prior = lax.axis_index("space") > 0
    rim_src = jnp.where(has_prior, both[1, :, 0, :], jnp.zeros_like(both[1, :, 0, :]))
    rim = remap_window(rim_src, upper_map, me * block - 1, block + 2)
    stacked = jnp.concatenate([rim[:, None], hidden_win[:, :, 1 : block + 3]], axis=1)
    pre2 = conv(stacked[None], w2, (1, 2))
    coarse_win = jax.nn.gelu(pre2 + b2[None, :, None, None]).astype(jnp.bfloat16)[0]

    hidden_part = hidden_win[:, :, halo - 1 : halo - 1 + block].reshape(groups, -1)
    coarse_part = coarse_win.reshape(groups, -1)
    back = lax.all_to_all(
        jnp.concatenate([hidden_part, coarse_part], 1).reshape(groups, 2, -1),
        "chan", 0, 0, tiled=True,
    ).reshape(groups, -1)
    h_len = hidden_part.shape[1]
    hidden_out = back[:, :h_len].reshape((groups, chans, rows, block))
    hidden_out = jnp.moveaxis(hidden_out, 0, 2).reshape(chans, rows, cycle)
    coarse_shape = coarse_win.shape
    coarse_out = back[:, h_len:].reshape(
        (groups, coarse_shape[0] // groups) + coarse_shape[1:]
    )
    coarse_out = jnp.moveaxis(coarse_out, 0, 2).reshape(
        (coarse_shape[0] // groups, coarse_shape[1], groups * coarse_shape[2])
    )
    return hidden_out[None], coarse_out[None]


def solution(mesh):
    placed = (
        P(None, "chan", "space", None),
        P("space", None),
        P("space", None),
        P("chan", None, None, None),
        P("chan"),
        P("chan", None, None, None),
        P("chan"),
    )
    return jax.shard_map(
        per_device,
        mesh=mesh,
        in_specs=placed,
        out_specs=(P(None, "chan", "space", None), P(None, "chan", "space", None)),
        check_vma=False,
    )
```

```python
import jax
import jax.numpy as jnp
from jax import lax
from jax.sharding import PartitionSpec as P


def shifted(array, axis, by):
    devices = lax.axis_size(axis)
    pairs = [(i, i + by) for i in range(devices) if 0 <= i + by < devices]
    return lax.ppermute(array, axis, pairs)


def rim_code(table, first_col, width):
    cycle = table.shape[0]
    cols = (first_col + jnp.arange(width)) % cycle
    picked = lax.dynamic_slice_in_dim(
        jnp.concatenate([table, table], axis=0), first_col % cycle, width, axis=0
    )
    code = jnp.where(picked == (cols + cycle - 1) % cycle, -1, 2)
    code = jnp.where(picked == (cols + 1) % cycle, 1, code)
    code = jnp.where(picked == cols, 0, code)
    return code.astype(jnp.bfloat16)


def apply_code(source, code):
    width = code.shape[0]
    same = source[..., 1 : width + 1]
    prev = source[..., 0:width]
    nxt = source[..., 2 : width + 2]
    zero = jnp.zeros_like(same)
    out = jnp.where(code == -1, prev, zero)
    out = jnp.where(code == 1, nxt, out)
    out = jnp.where(code == 0, same, out)
    return out


def remap_window(source, table, first_col, width):
    return apply_code(source, rim_code(table, first_col, width))


def remap_full(row, table):
    cycle = table.shape[0]
    wrapped = jnp.concatenate([row[..., -1:], row, row[..., :1]], axis=-1)
    return remap_window(wrapped, table, 0, cycle)


def split3(v):
    hi = lax.reduce_precision(v, exponent_bits=8, mantissa_bits=7)
    rest = v - hi
    mid = lax.reduce_precision(rest, exponent_bits=8, mantissa_bits=7)
    lo = rest - mid
    return jnp.stack([hi, mid, lo], -1).astype(jnp.bfloat16)


def join3(parts):
    parts = parts.astype(jnp.float32)
    return (parts[..., 0] + parts[..., 1]) + parts[..., 2]


def conv(x, w, stride):
    return lax.conv_general_dilated(
        x,
        w,
        window_strides=stride,
        padding="VALID",
        dimension_numbers=("NCHW", "OHWI", "NCHW"),
        preferred_element_type=jnp.float32,
    )


def column_windows(padded, groups, halo):
    cycle = padded.shape[-1]
    block = cycle // groups
    lead = padded.shape[:-1]
    left = jnp.roll(padded, halo, axis=-1).reshape(lead + (groups, block))[..., :halo]
    mid = padded.reshape(lead + (groups, block))
    right = jnp.roll(padded, -halo, axis=-1).reshape(lead + (groups, block))[..., block - halo :]
    wins = jnp.concatenate([left, mid, right], axis=-1)
    return jnp.moveaxis(wins, -2, 0)


def gather_low_bits(part, share):
    count = lax.axis_size("space")
    me = lax.axis_index("space")
    acc = part[None]
    bit = share // 2
    while bit >= 1:
        recv = lax.ppermute(acc, "space", [(i, i ^ bit) for i in range(count)])
        low = (me & bit) == 0
        pair = jnp.where(low, jnp.stack([acc, recv], 1), jnp.stack([recv, acc], 1))
        acc = pair.reshape((-1,) + part.shape)
        bit //= 2
    return acc


def pad_to(flat, multiple):
    extra = (-flat.shape[-1]) % multiple
    return jnp.pad(flat, [(0, 0)] * (flat.ndim - 1) + [(0, extra)])


def per_device(features, top_map, bottom_map, first_weight, first_bias, second_weight, second_bias):
    groups = lax.axis_size("chan")
    me = lax.axis_index("chan")
    x = features[0]
    chans = x.shape[0]
    rows = x.shape[1]
    cycle = x.shape[2]
    block = cycle // groups
    upper_map = top_map[0]
    lower_map = bottom_map[0]
    n1 = first_weight.shape[0]
    n2 = second_weight.shape[0]

    halo = 3
    width = block + 2 * halo
    wins = column_windows(x, groups, halo + 1).reshape(groups, -1)
    feat_len = wins.shape[1]

    flat_w = jnp.concatenate(
        [first_weight.reshape(n1, -1), second_weight.reshape(n2, -1)], axis=0
    )
    taps = flat_w.shape[1]
    packed_w = jnp.concatenate(
        [flat_w.reshape(-1), split3(jnp.concatenate([first_bias, second_bias])).reshape(-1)]
    )
    w_len = packed_w.shape[0]
    share = 4
    quarter = -(-w_len // (share * 128)) * 128
    packed_w = jnp.pad(packed_w, (0, share * quarter - w_len))
    where_me = lax.axis_index("space") % share
    mine = lax.dynamic_slice_in_dim(packed_w, where_me * quarter, quarter)
    sends = jnp.concatenate([wins, jnp.broadcast_to(mine[None], (groups, quarter))], 1)
    got = lax.all_to_all(
        pad_to(sends, 256).reshape(groups, 2, -1), "chan", 0, 0, tiled=True
    ).reshape(groups, -1)

    tile = got[:, :feat_len].reshape(groups * chans, rows, width + 2)
    pieces = gather_low_bits(got[:, feat_len : feat_len + quarter], share)
    every = jnp.moveaxis(pieces, 0, 1).reshape(groups, -1)
    w_all = every[:, : (n1 + n2) * taps].reshape(groups, n1 + n2, taps)
    b_all = every[:, (n1 + n2) * taps : w_len].reshape(groups, n1 + n2, 3)
    w1 = w_all[:, :n1].reshape((-1,) + first_weight.shape[1:])
    w2 = w_all[:, n1:].reshape((-1,) + second_weight.shape[1:])
    b1 = join3(b_all[:, :n1]).reshape(-1)
    b2 = join3(b_all[:, n1:]).reshape(-1)

    start = me * block - halo
    lower_code = rim_code(lower_map, start, width)
    code_rows = jnp.broadcast_to(jnp.pad(lower_code, (1, 1))[None, None], (1, rows, width + 2))
    prior_ext = shifted(jnp.concatenate([tile, code_rows], 0), "space", 1)
    prior = prior_ext[: groups * chans]
    prior_code = prior_ext[groups * chans, 0, 1 : width + 1]
    below_src = shifted(tile[:, 0, :], "space", -1)
    above = remap_window(prior[:, rows - 1, :], upper_map, start, width)
    below = apply_code(below_src, lower_code)
    prior_below = apply_code(tile[:, 0, :], prior_code)
    inner = tile[:, :, 1 : width + 1]
    prior_inner = prior[:, :, 1 : width + 1]
    window = jnp.stack(
        [
            jnp.concatenate([above[:, None], inner, below[:, None]], axis=1),
            jnp.concatenate([prior_inner, prior_below[:, None], prior_below[:, None]], axis=1),
        ],
        0,
    )

    pre1 = conv(window, w1, (1, 1))
    both = jax.nn.gelu(pre1 + b1[None, :, None, None]).astype(jnp.bfloat16)
    hidden_win = both[0]
    has_prior = lax.axis_index("space") > 0
    rim_src = jnp.where(has_prior, both[1, :, 0, :], jnp.zeros_like(both[1, :, 0, :]))
    rim = remap_window(rim_src, upper_map, me * block - 1, block + 2)
    stacked = jnp.concatenate([rim[:, None], hidden_win[:, :, 1 : block + 3]], axis=1)
    pre2 = conv(stacked[None], w2, (1, 2))
    coarse_win = jax.nn.gelu(pre2 + b2[None, :, None, None]).astype(jnp.bfloat16)[0]

    hidden_part = hidden_win[:, :, halo - 1 : halo - 1 + block].reshape(groups, -1)
    coarse_part = coarse_win.reshape(groups, -1)
    back = lax.all_to_all(
        jnp.concatenate([hidden_part, coarse_part], 1).reshape(groups, 2, -1),
        "chan", 0, 0, tiled=True,
    ).reshape(groups, -1)
    h_len = hidden_part.shape[1]
    hidden_out = back[:, :h_len].reshape((groups, chans, rows, block))
    hidden_out = jnp.moveaxis(hidden_out, 0, 2).reshape(chans, rows, cycle)
    coarse_shape = coarse_win.shape
    coarse_out = back[:, h_len:].reshape(
        (groups, coarse_shape[0] // groups) + coarse_shape[1:]
    )
    coarse_out = jnp.moveaxis(coarse_out, 0, 2).reshape(
        (coarse_shape[0] // groups, coarse_shape[1], groups * coarse_shape[2])
    )
    return hidden_out[None], coarse_out[None]


def solution(mesh):
    placed = (
        P(None, "chan", "space", None),
        P("space", None),
        P("space", None),
        P("chan", None, None, None),
        P("chan"),
        P("chan", None, None, None),
        P("chan"),
    )
    return jax.shard_map(
        per_device,
        mesh=mesh,
        in_specs=placed,
        out_specs=(P(None, "chan", "space", None), P(None, "chan", "space", None)),
        check_vma=False,
    )
```

```python
import jax
import jax.numpy as jnp
from jax import lax
from jax.sharding import PartitionSpec as P


def shifted(array, axis, by):
    devices = lax.axis_size(axis)
    pairs = [(i, i + by) for i in range(devices) if 0 <= i + by < devices]
    return lax.ppermute(array, axis, pairs)


def rim_code(table, first_col, width):
    cycle = table.shape[0]
    cols = (first_col + jnp.arange(width)) % cycle
    picked = lax.dynamic_slice_in_dim(
        jnp.concatenate([table, table], axis=0), first_col % cycle, width, axis=0
    )
    code = jnp.where(picked == (cols + cycle - 1) % cycle, -1, 2)
    code = jnp.where(picked == (cols + 1) % cycle, 1, code)
    code = jnp.where(picked == cols, 0, code)
    return code.astype(jnp.bfloat16)


def apply_code(source, code):
    width = code.shape[0]
    same = source[..., 1 : width + 1]
    prev = source[..., 0:width]
    nxt = source[..., 2 : width + 2]
    zero = jnp.zeros_like(same)
    out = jnp.where(code == -1, prev, zero)
    out = jnp.where(code == 1, nxt, out)
    out = jnp.where(code == 0, same, out)
    return out


def remap_window(source, table, first_col, width):
    return apply_code(source, rim_code(table, first_col, width))


def remap_full(row, table):
    cycle = table.shape[0]
    wrapped = jnp.concatenate([row[..., -1:], row, row[..., :1]], axis=-1)
    return remap_window(wrapped, table, 0, cycle)


def split3(v):
    hi = lax.reduce_precision(v, exponent_bits=8, mantissa_bits=7)
    rest = v - hi
    mid = lax.reduce_precision(rest, exponent_bits=8, mantissa_bits=7)
    lo = rest - mid
    return jnp.stack([hi, mid, lo], -1).astype(jnp.bfloat16)


def join3(parts):
    parts = parts.astype(jnp.float32)
    return (parts[..., 0] + parts[..., 1]) + parts[..., 2]


def conv(x, w, stride):
    return lax.conv_general_dilated(
        x,
        w,
        window_strides=stride,
        padding="VALID",
        dimension_numbers=("NCHW", "OHWI", "NCHW"),
        preferred_element_type=jnp.float32,
    )


def column_windows(padded, groups, halo):
    cycle = padded.shape[-1]
    block = cycle // groups
    lead = padded.shape[:-1]
    left = jnp.roll(padded, halo, axis=-1).reshape(lead + (groups, block))[..., :halo]
    mid = padded.reshape(lead + (groups, block))
    right = jnp.roll(padded, -halo, axis=-1).reshape(lead + (groups, block))[..., block - halo :]
    wins = jnp.concatenate([left, mid, right], axis=-1)
    return jnp.moveaxis(wins, -2, 0)


def pad_to(flat, multiple):
    extra = (-flat.shape[-1]) % multiple
    return jnp.pad(flat, [(0, 0)] * (flat.ndim - 1) + [(0, extra)])


def per_device(features, top_map, bottom_map, first_weight, first_bias, second_weight, second_bias):
    groups = lax.axis_size("chan")
    me = lax.axis_index("chan")
    x = features[0]
    chans = x.shape[0]
    rows = x.shape[1]
    cycle = x.shape[2]
    block = cycle // groups
    upper_map = top_map[0]
    lower_map = bottom_map[0]
    n1 = first_weight.shape[0]
    n2 = second_weight.shape[0]

    halo = 3
    width = block + 2 * halo
    wins = column_windows(x, groups, halo + 1).reshape(groups, -1)
    feat_len = wins.shape[1]

    flat_w = jnp.concatenate(
        [first_weight.reshape(n1, -1), second_weight.reshape(n2, -1)], axis=0
    )
    taps = flat_w.shape[1]
    packed_w = jnp.concatenate(
        [flat_w.reshape(-1), split3(jnp.concatenate([first_bias, second_bias])).reshape(-1)]
    )
    w_len = packed_w.shape[0]
    half = -(-w_len // 256) * 128
    packed_w = jnp.pad(packed_w, (0, 2 * half - w_len))
    second = (lax.axis_index("space") % 2) == 1
    mine = lax.dynamic_slice_in_dim(packed_w, jnp.where(second, half, 0), half)
    sends = jnp.concatenate([wins, jnp.broadcast_to(mine[None], (groups, half))], 1)
    got = lax.all_to_all(
        pad_to(sends, 256).reshape(groups, 2, -1), "chan", 0, 0, tiled=True
    ).reshape(groups, -1)

    tile = got[:, :feat_len].reshape(groups * chans, rows, width + 2)
    own_half = got[:, feat_len : feat_len + half]

    start = me * block - halo
    lower_code = rim_code(lower_map, start, width)
    line = rows * (width + 2)
    code_line = jnp.broadcast_to(jnp.pad(lower_code, (1, 1))[None], (rows, width + 2))
    w_lines = -(-own_half.size // line)
    w_flat = jnp.pad(own_half.reshape(-1), (0, w_lines * line - own_half.size))
    outgoing = jnp.concatenate(
        [tile.reshape(-1, line), code_line.reshape(1, line), w_flat.reshape(w_lines, line)], 0
    )
    spaces = lax.axis_size("space")
    incoming = lax.ppermute(outgoing, "space", [(i, (i + 1) % spaces) for i in range(spaces)])
    prior = incoming[: groups * chans].reshape(tile.shape)
    prior_code = incoming[groups * chans].reshape(rows, width + 2)[0, 1 : width + 1]
    other_half = incoming[groups * chans + 1 :].reshape(-1)[: own_half.size].reshape(own_half.shape)
    every = jnp.where(
        second,
        jnp.concatenate([other_half, own_half], 1),
        jnp.concatenate([own_half, other_half], 1),
    )
    w_all = every[:, : (n1 + n2) * taps].reshape(groups, n1 + n2, taps)
    b_all = every[:, (n1 + n2) * taps : w_len].reshape(groups, n1 + n2, 3)
    w1 = w_all[:, :n1].reshape((-1,) + first_weight.shape[1:])
    w2 = w_all[:, n1:].reshape((-1,) + second_weight.shape[1:])
    b1 = join3(b_all[:, :n1]).reshape(-1)
    b2 = join3(b_all[:, n1:]).reshape(-1)

    below_src = shifted(tile[:, 0, :], "space", -1)
    has_prior = lax.axis_index("space") > 0
    above = remap_window(prior[:, rows - 1, :], upper_map, start, width)
    above = jnp.where(has_prior, above, jnp.zeros_like(above))
    below = apply_code(below_src, lower_code)
    prior_below = apply_code(tile[:, 0, :], prior_code)
    inner = tile[:, :, 1 : width + 1]
    prior_inner = prior[:, :, 1 : width + 1]
    window = jnp.stack(
        [
            jnp.concatenate([above[:, None], inner, below[:, None]], axis=1),
            jnp.concatenate([prior_inner, prior_below[:, None], prior_below[:, None]], axis=1),
        ],
        0,
    )

    pre1 = conv(window, w1, (1, 1))
    both = jax.nn.gelu(pre1 + b1[None, :, None, None]).astype(jnp.bfloat16)
    hidden_win = both[0]
    rim_src = jnp.where(has_prior, both[1, :, 0, :], jnp.zeros_like(both[1, :, 0, :]))
    rim = remap_window(rim_src, upper_map, me * block - 1, block + 2)
    stacked = jnp.concatenate([rim[:, None], hidden_win[:, :, 1 : block + 3]], axis=1)
    pre2 = conv(stacked[None], w2, (1, 2))
    coarse_win = jax.nn.gelu(pre2 + b2[None, :, None, None]).astype(jnp.bfloat16)[0]

    hidden_part = hidden_win[:, :, halo - 1 : halo - 1 + block].reshape(groups, -1)
    coarse_part = coarse_win.reshape(groups, -1)
    back = lax.all_to_all(
        jnp.concatenate([hidden_part, coarse_part], 1).reshape(groups, 2, -1),
        "chan", 0, 0, tiled=True,
    ).reshape(groups, -1)
    h_len = hidden_part.shape[1]
    hidden_out = back[:, :h_len].reshape((groups, chans, rows, block))
    hidden_out = jnp.moveaxis(hidden_out, 0, 2).reshape(chans, rows, cycle)
    coarse_shape = coarse_win.shape
    coarse_out = back[:, h_len:].reshape(
        (groups, coarse_shape[0] // groups) + coarse_shape[1:]
    )
    coarse_out = jnp.moveaxis(coarse_out, 0, 2).reshape(
        (coarse_shape[0] // groups, coarse_shape[1], groups * coarse_shape[2])
    )
    return hidden_out[None], coarse_out[None]


def solution(mesh):
    placed = (
        P(None, "chan", "space", None),
        P("space", None),
        P("space", None),
        P("chan", None, None, None),
        P("chan"),
        P("chan", None, None, None),
        P("chan"),
    )
    return jax.shard_map(
        per_device,
        mesh=mesh,
        in_specs=placed,
        out_specs=(P(None, "chan", "space", None), P(None, "chan", "space", None)),
        check_vma=False,
    )
```

```python
import jax
import jax.numpy as jnp
from jax import lax
from jax.sharding import PartitionSpec as P


def shifted(array, axis, by):
    devices = lax.axis_size(axis)
    pairs = [(i, i + by) for i in range(devices) if 0 <= i + by < devices]
    return lax.ppermute(array, axis, pairs)


def rim_code(table, first_col, width):
    cycle = table.shape[0]
    cols = (first_col + jnp.arange(width)) % cycle
    picked = lax.dynamic_slice_in_dim(
        jnp.concatenate([table, table], axis=0), first_col % cycle, width, axis=0
    )
    code = jnp.where(picked == (cols + cycle - 1) % cycle, -1, 2)
    code = jnp.where(picked == (cols + 1) % cycle, 1, code)
    code = jnp.where(picked == cols, 0, code)
    return code.astype(jnp.bfloat16)


def apply_code(source, code):
    width = code.shape[0]
    same = source[..., 1 : width + 1]
    prev = source[..., 0:width]
    nxt = source[..., 2 : width + 2]
    zero = jnp.zeros_like(same)
    out = jnp.where(code == -1, prev, zero)
    out = jnp.where(code == 1, nxt, out)
    out = jnp.where(code == 0, same, out)
    return out


def remap_window(source, table, first_col, width):
    return apply_code(source, rim_code(table, first_col, width))


def remap_full(row, table):
    cycle = table.shape[0]
    wrapped = jnp.concatenate([row[..., -1:], row, row[..., :1]], axis=-1)
    return remap_window(wrapped, table, 0, cycle)


def split3(v):
    hi = lax.reduce_precision(v, exponent_bits=8, mantissa_bits=7)
    rest = v - hi
    mid = lax.reduce_precision(rest, exponent_bits=8, mantissa_bits=7)
    lo = rest - mid
    return jnp.stack([hi, mid, lo], -1).astype(jnp.bfloat16)


def join3(parts):
    parts = parts.astype(jnp.float32)
    return (parts[..., 0] + parts[..., 1]) + parts[..., 2]


def conv(x, w, stride):
    return lax.conv_general_dilated(
        x,
        w,
        window_strides=stride,
        padding="VALID",
        dimension_numbers=("NCHW", "OHWI", "NCHW"),
        preferred_element_type=jnp.float32,
    )


def column_windows(padded, groups, halo):
    cycle = padded.shape[-1]
    block = cycle // groups
    lead = padded.shape[:-1]
    mid = padded.reshape(lead + (groups, block))
    left = jnp.roll(mid[..., block - halo :], 1, axis=-2)
    right = jnp.roll(mid[..., :halo], -1, axis=-2)
    wins = jnp.concatenate([left, mid, right], axis=-1)
    return jnp.moveaxis(wins, -2, 0)


def pad_to(flat, multiple):
    extra = (-flat.shape[-1]) % multiple
    return jnp.pad(flat, [(0, 0)] * (flat.ndim - 1) + [(0, extra)])


def per_device(features, top_map, bottom_map, first_weight, first_bias, second_weight, second_bias):
    groups = lax.axis_size("chan")
    me = lax.axis_index("chan")
    x = features[0]
    chans = x.shape[0]
    rows = x.shape[1]
    cycle = x.shape[2]
    block = cycle // groups
    upper_map = top_map[0]
    lower_map = bottom_map[0]
    n1 = first_weight.shape[0]
    n2 = second_weight.shape[0]

    halo = 3
    width = block + 2 * halo
    wins = column_windows(x, groups, halo + 1).reshape(groups, -1)
    feat_len = wins.shape[1]

    flat_w = jnp.concatenate(
        [first_weight.reshape(n1, -1), second_weight.reshape(n2, -1)], axis=0
    )
    taps = flat_w.shape[1]
    packed_w = jnp.concatenate(
        [flat_w.reshape(-1), split3(jnp.concatenate([first_bias, second_bias])).reshape(-1)]
    )
    w_len = packed_w.shape[0]
    half = -(-w_len // 256) * 128
    packed_w = jnp.pad(packed_w, (0, 2 * half - w_len))
    second = (lax.axis_index("space") % 2) == 1
    mine = lax.dynamic_slice_in_dim(packed_w, jnp.where(second, half, 0), half)
    sends = jnp.concatenate([wins, jnp.broadcast_to(mine[None], (groups, half))], 1)
    got = lax.all_to_all(
        pad_to(sends, 256).reshape(groups, 2, -1), "chan", 0, 0, tiled=True
    ).reshape(groups, -1)

    tile = got[:, :feat_len].reshape(groups * chans, rows, width + 2)
    own_half = got[:, feat_len : feat_len + half]
    spaces = lax.axis_size("space")
    other_half = lax.ppermute(own_half, "space", [(i, i ^ 1) for i in range(spaces)])
    every = jnp.where(
        second,
        jnp.concatenate([other_half, own_half], 1),
        jnp.concatenate([own_half, other_half], 1),
    )
    w_all = every[:, : (n1 + n2) * taps].reshape(groups, n1 + n2, taps)
    b_all = every[:, (n1 + n2) * taps : w_len].reshape(groups, n1 + n2, 3)
    w1 = w_all[:, :n1].reshape((-1,) + first_weight.shape[1:])
    w2 = w_all[:, n1:].reshape((-1,) + second_weight.shape[1:])
    b1 = join3(b_all[:, :n1]).reshape(-1)
    b2 = join3(b_all[:, n1:]).reshape(-1)

    start = me * block - halo
    lower_code = rim_code(lower_map, start, width)
    code_rows = jnp.broadcast_to(jnp.pad(lower_code, (1, 1))[None, None], (1, rows, width + 2))
    prior_ext = shifted(jnp.concatenate([tile, code_rows], 0), "space", 1)
    prior = prior_ext[: groups * chans]
    prior_code = prior_ext[groups * chans, 0, 1 : width + 1]
    below_src = shifted(tile[:, 0, :], "space", -1)
    above = remap_window(prior[:, rows - 1, :], upper_map, start, width)
    below = apply_code(below_src, lower_code)
    prior_below = apply_code(tile[:, 0, :], prior_code)
    inner = tile[:, :, 1 : width + 1]
    prior_inner = prior[:, :, 1 : width + 1]
    window = jnp.stack(
        [
            jnp.concatenate([above[:, None], inner, below[:, None]], axis=1),
            jnp.concatenate([prior_inner, prior_below[:, None], prior_below[:, None]], axis=1),
        ],
        0,
    )

    pre1 = conv(window, w1, (1, 1))
    both = jax.nn.gelu(pre1 + b1[None, :, None, None]).astype(jnp.bfloat16)
    hidden_win = both[0]
    has_prior = lax.axis_index("space") > 0
    rim_src = jnp.where(has_prior, both[1, :, 0, :], jnp.zeros_like(both[1, :, 0, :]))
    rim = remap_window(rim_src, upper_map, me * block - 1, block + 2)
    stacked = jnp.concatenate([rim[:, None], hidden_win[:, :, 1 : block + 3]], axis=1)
    pre2 = conv(stacked[None], w2, (1, 2))
    coarse_win = jax.nn.gelu(pre2 + b2[None, :, None, None]).astype(jnp.bfloat16)[0]

    hidden_part = hidden_win[:, :, halo - 1 : halo - 1 + block].reshape(groups, -1)
    coarse_part = coarse_win.reshape(groups, -1)
    back = lax.all_to_all(
        jnp.concatenate([hidden_part, coarse_part], 1).reshape(groups, 2, -1),
        "chan", 0, 0, tiled=True,
    ).reshape(groups, -1)
    h_len = hidden_part.shape[1]
    hidden_out = back[:, :h_len].reshape((groups, chans, rows, block))
    hidden_out = jnp.moveaxis(hidden_out, 0, 2).reshape(chans, rows, cycle)
    coarse_shape = coarse_win.shape
    coarse_out = back[:, h_len:].reshape(
        (groups, coarse_shape[0] // groups) + coarse_shape[1:]
    )
    coarse_out = jnp.moveaxis(coarse_out, 0, 2).reshape(
        (coarse_shape[0] // groups, coarse_shape[1], groups * coarse_shape[2])
    )
    return hidden_out[None], coarse_out[None]


def solution(mesh):
    placed = (
        P(None, "chan", "space", None),
        P("space", None),
        P("space", None),
        P("chan", None, None, None),
        P("chan"),
        P("chan", None, None, None),
        P("chan"),
    )
    return jax.shard_map(
        per_device,
        mesh=mesh,
        in_specs=placed,
        out_specs=(P(None, "chan", "space", None), P(None, "chan", "space", None)),
        check_vma=False,
    )
```

```python
import jax
import jax.numpy as jnp
from jax import lax
from jax.sharding import PartitionSpec as P


def shifted(array, axis, by):
    devices = lax.axis_size(axis)
    pairs = [(i, i + by) for i in range(devices) if 0 <= i + by < devices]
    return lax.ppermute(array, axis, pairs)


def rim_code(table, first_col, width):
    cycle = table.shape[0]
    cols = (first_col + jnp.arange(width)) % cycle
    picked = lax.dynamic_slice_in_dim(
        jnp.concatenate([table, table], axis=0), first_col % cycle, width, axis=0
    )
    code = jnp.where(picked == (cols + cycle - 1) % cycle, -1, 2)
    code = jnp.where(picked == (cols + 1) % cycle, 1, code)
    code = jnp.where(picked == cols, 0, code)
    return code.astype(jnp.bfloat16)


def apply_code(source, code):
    width = code.shape[0]
    same = source[..., 1 : width + 1]
    prev = source[..., 0:width]
    nxt = source[..., 2 : width + 2]
    zero = jnp.zeros_like(same)
    out = jnp.where(code == -1, prev, zero)
    out = jnp.where(code == 1, nxt, out)
    out = jnp.where(code == 0, same, out)
    return out


def remap_window(source, table, first_col, width):
    return apply_code(source, rim_code(table, first_col, width))


def remap_full(row, table):
    cycle = table.shape[0]
    wrapped = jnp.concatenate([row[..., -1:], row, row[..., :1]], axis=-1)
    return remap_window(wrapped, table, 0, cycle)


def split3(v):
    hi = lax.reduce_precision(v, exponent_bits=8, mantissa_bits=7)
    rest = v - hi
    mid = lax.reduce_precision(rest, exponent_bits=8, mantissa_bits=7)
    lo = rest - mid
    return jnp.stack([hi, mid, lo], -1).astype(jnp.bfloat16)


def join3(parts):
    parts = parts.astype(jnp.float32)
    return (parts[..., 0] + parts[..., 1]) + parts[..., 2]


def conv(x, w, stride):
    return lax.conv_general_dilated(
        x,
        w,
        window_strides=stride,
        padding="VALID",
        dimension_numbers=("NCHW", "HWOI", "NCHW"),
        preferred_element_type=jnp.float32,
    )


def column_windows(padded, groups, halo):
    cycle = padded.shape[-1]
    block = cycle // groups
    lead = padded.shape[:-1]
    mid = padded.reshape(lead + (groups, block))
    left = jnp.roll(mid[..., block - halo :], 1, axis=-2)
    right = jnp.roll(mid[..., :halo], -1, axis=-2)
    wins = jnp.concatenate([left, mid, right], axis=-1)
    return jnp.moveaxis(wins, -2, 0)


def pad_to(flat, multiple):
    extra = (-flat.shape[-1]) % multiple
    return jnp.pad(flat, [(0, 0)] * (flat.ndim - 1) + [(0, extra)])


def per_device(features, top_map, bottom_map, first_weight, first_bias, second_weight, second_bias):
    groups = lax.axis_size("chan")
    me = lax.axis_index("chan")
    x = features[0]
    chans = x.shape[0]
    rows = x.shape[1]
    cycle = x.shape[2]
    block = cycle // groups
    upper_map = top_map[0]
    lower_map = bottom_map[0]
    n1 = first_weight.shape[0]
    n2 = second_weight.shape[0]

    halo = 3
    width = block + 2 * halo
    wins = column_windows(x, groups, halo + 1).reshape(groups, -1)
    feat_len = wins.shape[1]

    w1_len = first_weight.size
    w_total = w1_len + second_weight.size
    packed_w = jnp.concatenate(
        [
            jnp.transpose(first_weight, (1, 2, 0, 3)).reshape(-1),
            jnp.transpose(second_weight, (1, 2, 0, 3)).reshape(-1),
            split3(jnp.concatenate([first_bias, second_bias])).reshape(-1),
        ]
    )
    w_len = packed_w.shape[0]
    half = -(-w_len // 256) * 128
    packed_w = jnp.pad(packed_w, (0, 2 * half - w_len))
    second = (lax.axis_index("space") % 2) == 1
    mine = lax.dynamic_slice_in_dim(packed_w, jnp.where(second, half, 0), half)
    sends = jnp.concatenate([wins, jnp.broadcast_to(mine[None], (groups, half))], 1)
    got = lax.all_to_all(
        pad_to(sends, 256).reshape(groups, 2, -1), "chan", 0, 0, tiled=True
    ).reshape(groups, -1)

    tile = got[:, :feat_len].reshape(groups * chans, rows, width + 2)
    own_half = got[:, feat_len : feat_len + half]
    spaces = lax.axis_size("space")
    other_half = lax.ppermute(own_half, "space", [(i, i ^ 1) for i in range(spaces)])
    every = jnp.where(
        second,
        jnp.concatenate([other_half, own_half], 1),
        jnp.concatenate([own_half, other_half], 1),
    )
    k1 = first_weight.shape[1:3]
    k2 = second_weight.shape[1:3]
    w1 = every[:, :w1_len].reshape((groups,) + k1 + (n1, first_weight.shape[3]))
    w1 = jnp.moveaxis(w1, 0, 2).reshape(k1 + (groups * n1, first_weight.shape[3]))
    w2 = every[:, w1_len:w_total].reshape((groups,) + k2 + (n2, second_weight.shape[3]))
    w2 = jnp.moveaxis(w2, 0, 2).reshape(k2 + (groups * n2, second_weight.shape[3]))
    b_all = every[:, w_total:w_len].reshape(groups, n1 + n2, 3)
    b1 = join3(b_all[:, :n1]).reshape(-1)
    b2 = join3(b_all[:, n1:]).reshape(-1)

    start = me * block - halo
    lower_code = rim_code(lower_map, start, width)
    code_rows = jnp.broadcast_to(jnp.pad(lower_code, (1, 1))[None, None], (1, rows, width + 2))
    prior_ext = shifted(jnp.concatenate([tile, code_rows], 0), "space", 1)
    prior = prior_ext[: groups * chans]
    prior_code = prior_ext[groups * chans, 0, 1 : width + 1]
    below_src = shifted(tile[:, 0, :], "space", -1)
    above = remap_window(prior[:, rows - 1, :], upper_map, start, width)
    below = apply_code(below_src, lower_code)
    prior_below = apply_code(tile[:, 0, :], prior_code)
    inner = tile[:, :, 1 : width + 1]
    prior_inner = prior[:, :, 1 : width + 1]
    window = jnp.stack(
        [
            jnp.concatenate([above[:, None], inner, below[:, None]], axis=1),
            jnp.concatenate([prior_inner, prior_below[:, None], prior_below[:, None]], axis=1),
        ],
        0,
    )

    pre1 = conv(window, w1, (1, 1))
    both = jax.nn.gelu(pre1 + b1[None, :, None, None]).astype(jnp.bfloat16)
    hidden_win = both[0]
    has_prior = lax.axis_index("space") > 0
    rim_src = jnp.where(has_prior, both[1, :, 0, :], jnp.zeros_like(both[1, :, 0, :]))
    rim = remap_window(rim_src, upper_map, me * block - 1, block + 2)
    stacked = jnp.concatenate([rim[:, None], hidden_win[:, :, 1 : block + 3]], axis=1)
    pre2 = conv(stacked[None], w2, (1, 2))
    coarse_win = jax.nn.gelu(pre2 + b2[None, :, None, None]).astype(jnp.bfloat16)[0]

    hidden_part = hidden_win[:, :, halo - 1 : halo - 1 + block].reshape(groups, -1)
    coarse_part = coarse_win.reshape(groups, -1)
    back = lax.all_to_all(
        jnp.concatenate([hidden_part, coarse_part], 1).reshape(groups, 2, -1),
        "chan", 0, 0, tiled=True,
    ).reshape(groups, -1)
    h_len = hidden_part.shape[1]
    hidden_out = back[:, :h_len].reshape((groups, chans, rows, block))
    hidden_out = jnp.moveaxis(hidden_out, 0, 2).reshape(chans, rows, cycle)
    coarse_shape = coarse_win.shape
    coarse_out = back[:, h_len:].reshape(
        (groups, coarse_shape[0] // groups) + coarse_shape[1:]
    )
    coarse_out = jnp.moveaxis(coarse_out, 0, 2).reshape(
        (coarse_shape[0] // groups, coarse_shape[1], groups * coarse_shape[2])
    )
    return hidden_out[None], coarse_out[None]


def solution(mesh):
    placed = (
        P(None, "chan", "space", None),
        P("space", None),
        P("space", None),
        P("chan", None, None, None),
        P("chan"),
        P("chan", None, None, None),
        P("chan"),
    )
    return jax.shard_map(
        per_device,
        mesh=mesh,
        in_specs=placed,
        out_specs=(P(None, "chan", "space", None), P(None, "chan", "space", None)),
        check_vma=False,
    )
```

```python
import jax
import jax.numpy as jnp
from jax import lax
from jax.sharding import PartitionSpec as P


def shifted(array, axis, by):
    devices = lax.axis_size(axis)
    pairs = [(i, i + by) for i in range(devices) if 0 <= i + by < devices]
    return lax.ppermute(array, axis, pairs)


def rim_code(table, first_col, width):
    cycle = table.shape[0]
    cols = (first_col + jnp.arange(width)) % cycle
    picked = lax.dynamic_slice_in_dim(
        jnp.concatenate([table, table], axis=0), first_col % cycle, width, axis=0
    )
    code = jnp.where(picked == (cols + cycle - 1) % cycle, -1, 2)
    code = jnp.where(picked == (cols + 1) % cycle, 1, code)
    code = jnp.where(picked == cols, 0, code)
    return code.astype(jnp.bfloat16)


def apply_code(source, code):
    width = code.shape[0]
    same = source[..., 1 : width + 1]
    prev = source[..., 0:width]
    nxt = source[..., 2 : width + 2]
    zero = jnp.zeros_like(same)
    out = jnp.where(code == -1, prev, zero)
    out = jnp.where(code == 1, nxt, out)
    out = jnp.where(code == 0, same, out)
    return out


def remap_window(source, table, first_col, width):
    return apply_code(source, rim_code(table, first_col, width))


def remap_full(row, table):
    cycle = table.shape[0]
    wrapped = jnp.concatenate([row[..., -1:], row, row[..., :1]], axis=-1)
    return remap_window(wrapped, table, 0, cycle)


def split3(v):
    hi = lax.reduce_precision(v, exponent_bits=8, mantissa_bits=7)
    rest = v - hi
    mid = lax.reduce_precision(rest, exponent_bits=8, mantissa_bits=7)
    lo = rest - mid
    return jnp.stack([hi, mid, lo], -1).astype(jnp.bfloat16)


def join3(parts):
    parts = parts.astype(jnp.float32)
    return (parts[..., 0] + parts[..., 1]) + parts[..., 2]


def conv(x, w, stride):
    return lax.conv_general_dilated(
        x,
        w,
        window_strides=stride,
        padding="VALID",
        dimension_numbers=("NCHW", "HWOI", "NCHW"),
        preferred_element_type=jnp.float32,
    )


def column_windows(padded, groups, halo):
    cycle = padded.shape[-1]
    block = cycle // groups
    lead = padded.shape[:-1]
    mid = padded.reshape(lead + (groups, block))
    left = jnp.roll(mid[..., block - halo :], 1, axis=-2)
    right = jnp.roll(mid[..., :halo], -1, axis=-2)
    wins = jnp.concatenate([left, mid, right], axis=-1)
    return jnp.moveaxis(wins, -2, 0)


def gather_low_bits(part, share):
    count = lax.axis_size("space")
    me = lax.axis_index("space")
    acc = part[None]
    bit = share // 2
    while bit >= 1:
        recv = lax.ppermute(acc, "space", [(i, i ^ bit) for i in range(count)])
        low = (me & bit) == 0
        pair = jnp.where(low, jnp.stack([acc, recv], 1), jnp.stack([recv, acc], 1))
        acc = pair.reshape((-1,) + part.shape)
        bit //= 2
    return acc


def pad_to(flat, multiple):
    extra = (-flat.shape[-1]) % multiple
    return jnp.pad(flat, [(0, 0)] * (flat.ndim - 1) + [(0, extra)])


def per_device(features, top_map, bottom_map, first_weight, first_bias, second_weight, second_bias):
    groups = lax.axis_size("chan")
    me = lax.axis_index("chan")
    x = features[0]
    chans = x.shape[0]
    rows = x.shape[1]
    cycle = x.shape[2]
    block = cycle // groups
    upper_map = top_map[0]
    lower_map = bottom_map[0]
    n1 = first_weight.shape[0]
    n2 = second_weight.shape[0]

    halo = 3
    width = block + 2 * halo
    wins = column_windows(x, groups, halo + 1).reshape(groups, -1)
    feat_len = wins.shape[1]

    w1_len = first_weight.size
    w_total = w1_len + second_weight.size
    packed_w = jnp.concatenate(
        [
            jnp.transpose(first_weight, (1, 2, 0, 3)).reshape(-1),
            jnp.transpose(second_weight, (1, 2, 0, 3)).reshape(-1),
            split3(jnp.concatenate([first_bias, second_bias])).reshape(-1),
        ]
    )
    w_len = packed_w.shape[0]
    share = 4
    quarter = -(-w_len // (share * 128)) * 128
    packed_w = jnp.pad(packed_w, (0, share * quarter - w_len))
    where_me = lax.axis_index("space") % share
    mine = lax.dynamic_slice_in_dim(packed_w, where_me * quarter, quarter)
    sends = jnp.concatenate([wins, jnp.broadcast_to(mine[None], (groups, quarter))], 1)
    got = lax.all_to_all(
        pad_to(sends, 256).reshape(groups, 2, -1), "chan", 0, 0, tiled=True
    ).reshape(groups, -1)

    tile = got[:, :feat_len].reshape(groups * chans, rows, width + 2)
    pieces = gather_low_bits(got[:, feat_len : feat_len + quarter], share)
    every = jnp.moveaxis(pieces, 0, 1).reshape(groups, -1)
    k1 = first_weight.shape[1:3]
    k2 = second_weight.shape[1:3]
    w1 = every[:, :w1_len].reshape((groups,) + k1 + (n1, first_weight.shape[3]))
    w1 = jnp.moveaxis(w1, 0, 2).reshape(k1 + (groups * n1, first_weight.shape[3]))
    w2 = every[:, w1_len:w_total].reshape((groups,) + k2 + (n2, second_weight.shape[3]))
    w2 = jnp.moveaxis(w2, 0, 2).reshape(k2 + (groups * n2, second_weight.shape[3]))
    b_all = every[:, w_total:w_len].reshape(groups, n1 + n2, 3)
    b1 = join3(b_all[:, :n1]).reshape(-1)
    b2 = join3(b_all[:, n1:]).reshape(-1)

    start = me * block - halo
    lower_code = rim_code(lower_map, start, width)
    code_rows = jnp.broadcast_to(jnp.pad(lower_code, (1, 1))[None, None], (1, rows, width + 2))
    prior_ext = shifted(jnp.concatenate([tile, code_rows], 0), "space", 1)
    prior = prior_ext[: groups * chans]
    prior_code = prior_ext[groups * chans, 0, 1 : width + 1]
    below_src = shifted(tile[:, 0, :], "space", -1)
    above = remap_window(prior[:, rows - 1, :], upper_map, start, width)
    below = apply_code(below_src, lower_code)
    prior_below = apply_code(tile[:, 0, :], prior_code)
    inner = tile[:, :, 1 : width + 1]
    prior_inner = prior[:, :, 1 : width + 1]
    window = jnp.stack(
        [
            jnp.concatenate([above[:, None], inner, below[:, None]], axis=1),
            jnp.concatenate([prior_inner, prior_below[:, None], prior_below[:, None]], axis=1),
        ],
        0,
    )

    pre1 = conv(window, w1, (1, 1))
    both = jax.nn.gelu(pre1 + b1[None, :, None, None]).astype(jnp.bfloat16)
    hidden_win = both[0]
    has_prior = lax.axis_index("space") > 0
    rim_src = jnp.where(has_prior, both[1, :, 0, :], jnp.zeros_like(both[1, :, 0, :]))
    rim = remap_window(rim_src, upper_map, me * block - 1, block + 2)
    stacked = jnp.concatenate([rim[:, None], hidden_win[:, :, 1 : block + 3]], axis=1)
    pre2 = conv(stacked[None], w2, (1, 2))
    coarse_win = jax.nn.gelu(pre2 + b2[None, :, None, None]).astype(jnp.bfloat16)[0]

    hidden_part = hidden_win[:, :, halo - 1 : halo - 1 + block].reshape(groups, -1)
    coarse_part = coarse_win.reshape(groups, -1)
    back = lax.all_to_all(
        jnp.concatenate([hidden_part, coarse_part], 1).reshape(groups, 2, -1),
        "chan", 0, 0, tiled=True,
    ).reshape(groups, -1)
    h_len = hidden_part.shape[1]
    hidden_out = back[:, :h_len].reshape((groups, chans, rows, block))
    hidden_out = jnp.moveaxis(hidden_out, 0, 2).reshape(chans, rows, cycle)
    coarse_shape = coarse_win.shape
    coarse_out = back[:, h_len:].reshape(
        (groups, coarse_shape[0] // groups) + coarse_shape[1:]
    )
    coarse_out = jnp.moveaxis(coarse_out, 0, 2).reshape(
        (coarse_shape[0] // groups, coarse_shape[1], groups * coarse_shape[2])
    )
    return hidden_out[None], coarse_out[None]


def solution(mesh):
    placed = (
        P(None, "chan", "space", None),
        P("space", None),
        P("space", None),
        P("chan", None, None, None),
        P("chan"),
        P("chan", None, None, None),
        P("chan"),
    )
    return jax.shard_map(
        per_device,
        mesh=mesh,
        in_specs=placed,
        out_specs=(P(None, "chan", "space", None), P(None, "chan", "space", None)),
        check_vma=False,
    )
```

```python
import jax
import jax.numpy as jnp
from jax import lax
from jax.sharding import PartitionSpec as P


def shifted(array, axis, by):
    devices = lax.axis_size(axis)
    pairs = [(i, i + by) for i in range(devices) if 0 <= i + by < devices]
    return lax.ppermute(array, axis, pairs)


def rim_code(table, first_col, width):
    cycle = table.shape[0]
    cols = (first_col + jnp.arange(width)) % cycle
    picked = lax.dynamic_slice_in_dim(
        jnp.concatenate([table, table], axis=0), first_col % cycle, width, axis=0
    )
    code = jnp.where(picked == (cols + cycle - 1) % cycle, -1, 2)
    code = jnp.where(picked == (cols + 1) % cycle, 1, code)
    code = jnp.where(picked == cols, 0, code)
    return code.astype(jnp.bfloat16)


def apply_code(source, code):
    width = code.shape[0]
    same = source[..., 1 : width + 1]
    prev = source[..., 0:width]
    nxt = source[..., 2 : width + 2]
    zero = jnp.zeros_like(same)
    out = jnp.where(code == -1, prev, zero)
    out = jnp.where(code == 1, nxt, out)
    out = jnp.where(code == 0, same, out)
    return out


def remap_window(source, table, first_col, width):
    return apply_code(source, rim_code(table, first_col, width))


def remap_full(row, table):
    cycle = table.shape[0]
    wrapped = jnp.concatenate([row[..., -1:], row, row[..., :1]], axis=-1)
    return remap_window(wrapped, table, 0, cycle)


def split3(v):
    hi = lax.reduce_precision(v, exponent_bits=8, mantissa_bits=7)
    rest = v - hi
    mid = lax.reduce_precision(rest, exponent_bits=8, mantissa_bits=7)
    lo = rest - mid
    return jnp.stack([hi, mid, lo], -1).astype(jnp.bfloat16)


def join3(parts):
    parts = parts.astype(jnp.float32)
    return (parts[..., 0] + parts[..., 1]) + parts[..., 2]


def conv(x, w, stride):
    return lax.conv_general_dilated(
        x,
        w,
        window_strides=stride,
        padding="VALID",
        dimension_numbers=("NCHW", "HWOI", "NCHW"),
        preferred_element_type=jnp.float32,
    )


def column_windows(padded, groups, halo):
    cycle = padded.shape[-1]
    block = cycle // groups
    lead = padded.shape[:-1]
    mid = padded.reshape(lead + (groups, block))
    left = jnp.roll(mid[..., block - halo :], 1, axis=-2)
    right = jnp.roll(mid[..., :halo], -1, axis=-2)
    wins = jnp.concatenate([left, mid, right], axis=-1)
    return jnp.moveaxis(wins, -2, 0)


def gather_low_bits(part, share):
    count = lax.axis_size("space")
    me = lax.axis_index("space")
    acc = part[None]
    bit = share // 2
    while bit >= 1:
        recv = lax.ppermute(acc, "space", [(i, i ^ bit) for i in range(count)])
        low = (me & bit) == 0
        pair = jnp.where(low, jnp.stack([acc, recv], 1), jnp.stack([recv, acc], 1))
        acc = pair.reshape((-1,) + part.shape)
        bit //= 2
    return acc


def pad_to(flat, multiple):
    extra = (-flat.shape[-1]) % multiple
    return jnp.pad(flat, [(0, 0)] * (flat.ndim - 1) + [(0, extra)])


def per_device(features, top_map, bottom_map, first_weight, first_bias, second_weight, second_bias):
    groups = lax.axis_size("chan")
    me = lax.axis_index("chan")
    x = features[0]
    chans = x.shape[0]
    rows = x.shape[1]
    cycle = x.shape[2]
    block = cycle // groups
    upper_map = top_map[0]
    lower_map = bottom_map[0]
    n1 = first_weight.shape[0]
    n2 = second_weight.shape[0]

    halo = 3
    width = block + 2 * halo
    wins = column_windows(x, groups, halo + 1).reshape(groups, -1)
    feat_len = wins.shape[1]

    w1_len = first_weight.size
    w_total = w1_len + second_weight.size
    packed_w = jnp.concatenate(
        [
            jnp.transpose(first_weight, (1, 2, 0, 3)).reshape(-1),
            jnp.transpose(second_weight, (1, 2, 0, 3)).reshape(-1),
            split3(jnp.concatenate([first_bias, second_bias])).reshape(-1),
        ]
    )
    w_len = packed_w.shape[0]
    share = 8
    quarter = -(-w_len // (share * 128)) * 128
    packed_w = jnp.pad(packed_w, (0, share * quarter - w_len))
    where_me = lax.axis_index("space") % share
    mine = lax.dynamic_slice_in_dim(packed_w, where_me * quarter, quarter)
    sends = jnp.concatenate([wins, jnp.broadcast_to(mine[None], (groups, quarter))], 1)
    got = lax.all_to_all(
        pad_to(sends, 256).reshape(groups, 2, -1), "chan", 0, 0, tiled=True
    ).reshape(groups, -1)

    tile = got[:, :feat_len].reshape(groups * chans, rows, width + 2)
    pieces = gather_low_bits(got[:, feat_len : feat_len + quarter], share)
    every = jnp.moveaxis(pieces, 0, 1).reshape(groups, -1)
    k1 = first_weight.shape[1:3]
    k2 = second_weight.shape[1:3]
    w1 = every[:, :w1_len].reshape((groups,) + k1 + (n1, first_weight.shape[3]))
    w1 = jnp.moveaxis(w1, 0, 2).reshape(k1 + (groups * n1, first_weight.shape[3]))
    w2 = every[:, w1_len:w_total].reshape((groups,) + k2 + (n2, second_weight.shape[3]))
    w2 = jnp.moveaxis(w2, 0, 2).reshape(k2 + (groups * n2, second_weight.shape[3]))
    b_all = every[:, w_total:w_len].reshape(groups, n1 + n2, 3)
    b1 = join3(b_all[:, :n1]).reshape(-1)
    b2 = join3(b_all[:, n1:]).reshape(-1)

    start = me * block - halo
    lower_code = rim_code(lower_map, start, width)
    code_rows = jnp.broadcast_to(jnp.pad(lower_code, (1, 1))[None, None], (1, rows, width + 2))
    prior_ext = shifted(jnp.concatenate([tile, code_rows], 0), "space", 1)
    prior = prior_ext[: groups * chans]
    prior_code = prior_ext[groups * chans, 0, 1 : width + 1]
    below_src = shifted(tile[:, 0, :], "space", -1)
    above = remap_window(prior[:, rows - 1, :], upper_map, start, width)
    below = apply_code(below_src, lower_code)
    prior_below = apply_code(tile[:, 0, :], prior_code)
    inner = tile[:, :, 1 : width + 1]
    prior_inner = prior[:, :, 1 : width + 1]
    window = jnp.stack(
        [
            jnp.concatenate([above[:, None], inner, below[:, None]], axis=1),
            jnp.concatenate([prior_inner, prior_below[:, None], prior_below[:, None]], axis=1),
        ],
        0,
    )

    pre1 = conv(window, w1, (1, 1))
    both = jax.nn.gelu(pre1 + b1[None, :, None, None]).astype(jnp.bfloat16)
    hidden_win = both[0]
    has_prior = lax.axis_index("space") > 0
    rim_src = jnp.where(has_prior, both[1, :, 0, :], jnp.zeros_like(both[1, :, 0, :]))
    rim = remap_window(rim_src, upper_map, me * block - 1, block + 2)
    stacked = jnp.concatenate([rim[:, None], hidden_win[:, :, 1 : block + 3]], axis=1)
    pre2 = conv(stacked[None], w2, (1, 2))
    coarse_win = jax.nn.gelu(pre2 + b2[None, :, None, None]).astype(jnp.bfloat16)[0]

    hidden_part = hidden_win[:, :, halo - 1 : halo - 1 + block].reshape(groups, -1)
    coarse_part = coarse_win.reshape(groups, -1)
    back = lax.all_to_all(
        jnp.concatenate([hidden_part, coarse_part], 1).reshape(groups, 2, -1),
        "chan", 0, 0, tiled=True,
    ).reshape(groups, -1)
    h_len = hidden_part.shape[1]
    hidden_out = back[:, :h_len].reshape((groups, chans, rows, block))
    hidden_out = jnp.moveaxis(hidden_out, 0, 2).reshape(chans, rows, cycle)
    coarse_shape = coarse_win.shape
    coarse_out = back[:, h_len:].reshape(
        (groups, coarse_shape[0] // groups) + coarse_shape[1:]
    )
    coarse_out = jnp.moveaxis(coarse_out, 0, 2).reshape(
        (coarse_shape[0] // groups, coarse_shape[1], groups * coarse_shape[2])
    )
    return hidden_out[None], coarse_out[None]


def solution(mesh):
    placed = (
        P(None, "chan", "space", None),
        P("space", None),
        P("space", None),
        P("chan", None, None, None),
        P("chan"),
        P("chan", None, None, None),
        P("chan"),
    )
    return jax.shard_map(
        per_device,
        mesh=mesh,
        in_specs=placed,
        out_specs=(P(None, "chan", "space", None), P(None, "chan", "space", None)),
        check_vma=False,
    )
```

```python
import jax
import jax.numpy as jnp
from jax import lax
from jax.sharding import PartitionSpec as P


def shifted(array, axis, by):
    devices = lax.axis_size(axis)
    pairs = [(i, i + by) for i in range(devices) if 0 <= i + by < devices]
    return lax.ppermute(array, axis, pairs)


def rim_code(table, first_col, width):
    cycle = table.shape[0]
    cols = (first_col + jnp.arange(width)) % cycle
    picked = lax.dynamic_slice_in_dim(
        jnp.concatenate([table, table], axis=0), first_col % cycle, width, axis=0
    )
    code = jnp.where(picked == (cols + cycle - 1) % cycle, -1, 2)
    code = jnp.where(picked == (cols + 1) % cycle, 1, code)
    code = jnp.where(picked == cols, 0, code)
    return code.astype(jnp.bfloat16)


def apply_code(source, code):
    width = code.shape[0]
    same = source[..., 1 : width + 1]
    prev = source[..., 0:width]
    nxt = source[..., 2 : width + 2]
    zero = jnp.zeros_like(same)
    out = jnp.where(code == -1, prev, zero)
    out = jnp.where(code == 1, nxt, out)
    out = jnp.where(code == 0, same, out)
    return out


def remap_window(source, table, first_col, width):
    return apply_code(source, rim_code(table, first_col, width))


def remap_full(row, table):
    cycle = table.shape[0]
    wrapped = jnp.concatenate([row[..., -1:], row, row[..., :1]], axis=-1)
    return remap_window(wrapped, table, 0, cycle)


def split3(v):
    hi = lax.reduce_precision(v, exponent_bits=8, mantissa_bits=7)
    rest = v - hi
    mid = lax.reduce_precision(rest, exponent_bits=8, mantissa_bits=7)
    lo = rest - mid
    return jnp.stack([hi, mid, lo], -1).astype(jnp.bfloat16)


def join3(parts):
    parts = parts.astype(jnp.float32)
    return (parts[..., 0] + parts[..., 1]) + parts[..., 2]


def conv(x, w, stride):
    return lax.conv_general_dilated(
        x,
        w,
        window_strides=stride,
        padding="VALID",
        dimension_numbers=("NCHW", "HWOI", "NCHW"),
        preferred_element_type=jnp.float32,
    )


def column_windows(padded, groups, halo):
    cycle = padded.shape[-1]
    block = cycle // groups
    lead = padded.shape[:-1]
    mid = padded.reshape(lead + (groups, block))
    left = jnp.roll(mid[..., block - halo :], 1, axis=-2)
    right = jnp.roll(mid[..., :halo], -1, axis=-2)
    wins = jnp.concatenate([left, mid, right], axis=-1)
    return jnp.moveaxis(wins, -2, 0)


def gather_low_bits(part, share):
    count = lax.axis_size("space")
    me = lax.axis_index("space")
    acc = part[None]
    bit = share // 2
    while bit >= 1:
        recv = lax.ppermute(acc, "space", [(i, i ^ bit) for i in range(count)])
        low = (me & bit) == 0
        pair = jnp.where(low, jnp.stack([acc, recv], 1), jnp.stack([recv, acc], 1))
        acc = pair.reshape((-1,) + part.shape)
        bit //= 2
    return acc


def pad_to(flat, multiple):
    extra = (-flat.shape[-1]) % multiple
    return jnp.pad(flat, [(0, 0)] * (flat.ndim - 1) + [(0, extra)])


def per_device(features, top_map, bottom_map, first_weight, first_bias, second_weight, second_bias):
    groups = lax.axis_size("chan")
    me = lax.axis_index("chan")
    x = features[0]
    chans = x.shape[0]
    rows = x.shape[1]
    cycle = x.shape[2]
    block = cycle // groups
    upper_map = top_map[0]
    lower_map = bottom_map[0]
    n1 = first_weight.shape[0]
    n2 = second_weight.shape[0]

    halo = 3
    width = block + 2 * halo
    wins = column_windows(x, groups, halo + 1).reshape(groups, -1)
    feat_len = wins.shape[1]

    head = jnp.concatenate(
        [
            jnp.transpose(first_weight, (1, 2, 0, 3)).reshape(-1),
            split3(jnp.concatenate([first_bias, second_bias])).reshape(-1),
        ]
    )
    head = jnp.pad(head, (0, (-head.shape[0]) % 128))
    tail = jnp.transpose(second_weight, (1, 2, 0, 3)).reshape(-1)
    share = 4
    quarter = -(-tail.shape[0] // (share * 128)) * 128
    tail = jnp.pad(tail, (0, share * quarter - tail.shape[0]))
    where_me = lax.axis_index("space") % share
    mine = jnp.concatenate([head, lax.dynamic_slice_in_dim(tail, where_me * quarter, quarter)])
    sends = jnp.concatenate([wins, jnp.broadcast_to(mine[None], (groups, mine.shape[0]))], 1)
    got = lax.all_to_all(
        pad_to(sends, 256).reshape(groups, 2, -1), "chan", 0, 0, tiled=True
    ).reshape(groups, -1)

    tile = got[:, :feat_len].reshape(groups * chans, rows, width + 2)
    heads = got[:, feat_len : feat_len + head.shape[0]]
    pieces = gather_low_bits(got[:, feat_len + head.shape[0] : feat_len + mine.shape[0]], share)
    tails = jnp.moveaxis(pieces, 0, 1).reshape(groups, -1)
    k1 = first_weight.shape[1:3]
    k2 = second_weight.shape[1:3]
    w1_len = first_weight.size
    w1 = heads[:, :w1_len].reshape((groups,) + k1 + (n1, first_weight.shape[3]))
    w1 = jnp.moveaxis(w1, 0, 2).reshape(k1 + (groups * n1, first_weight.shape[3]))
    b_all = heads[:, w1_len : w1_len + (n1 + n2) * 3].reshape(groups, n1 + n2, 3)
    w2 = tails[:, : second_weight.size].reshape((groups,) + k2 + (n2, second_weight.shape[3]))
    w2 = jnp.moveaxis(w2, 0, 2).reshape(k2 + (groups * n2, second_weight.shape[3]))
    b1 = join3(b_all[:, :n1]).reshape(-1)
    b2 = join3(b_all[:, n1:]).reshape(-1)

    start = me * block - halo
    lower_code = rim_code(lower_map, start, width)
    code_rows = jnp.broadcast_to(jnp.pad(lower_code, (1, 1))[None, None], (1, rows, width + 2))
    prior_ext = shifted(jnp.concatenate([tile, code_rows], 0), "space", 1)
    prior = prior_ext[: groups * chans]
    prior_code = prior_ext[groups * chans, 0, 1 : width + 1]
    below_src = shifted(tile[:, 0, :], "space", -1)
    above = remap_window(prior[:, rows - 1, :], upper_map, start, width)
    below = apply_code(below_src, lower_code)
    prior_below = apply_code(tile[:, 0, :], prior_code)
    inner = tile[:, :, 1 : width + 1]
    prior_inner = prior[:, :, 1 : width + 1]
    window = jnp.stack(
        [
            jnp.concatenate([above[:, None], inner, below[:, None]], axis=1),
            jnp.concatenate([prior_inner, prior_below[:, None], prior_below[:, None]], axis=1),
        ],
        0,
    )

    pre1 = conv(window, w1, (1, 1))
    both = jax.nn.gelu(pre1 + b1[None, :, None, None]).astype(jnp.bfloat16)
    hidden_win = both[0]
    has_prior = lax.axis_index("space") > 0
    rim_src = jnp.where(has_prior, both[1, :, 0, :], jnp.zeros_like(both[1, :, 0, :]))
    rim = remap_window(rim_src, upper_map, me * block - 1, block + 2)
    stacked = jnp.concatenate([rim[:, None], hidden_win[:, :, 1 : block + 3]], axis=1)
    pre2 = conv(stacked[None], w2, (1, 2))
    coarse_win = jax.nn.gelu(pre2 + b2[None, :, None, None]).astype(jnp.bfloat16)[0]

    hidden_part = hidden_win[:, :, halo - 1 : halo - 1 + block].reshape(groups, -1)
    coarse_part = coarse_win.reshape(groups, -1)
    back = lax.all_to_all(
        jnp.concatenate([hidden_part, coarse_part], 1).reshape(groups, 2, -1),
        "chan", 0, 0, tiled=True,
    ).reshape(groups, -1)
    h_len = hidden_part.shape[1]
    hidden_out = back[:, :h_len].reshape((groups, chans, rows, block))
    hidden_out = jnp.moveaxis(hidden_out, 0, 2).reshape(chans, rows, cycle)
    coarse_shape = coarse_win.shape
    coarse_out = back[:, h_len:].reshape(
        (groups, coarse_shape[0] // groups) + coarse_shape[1:]
    )
    coarse_out = jnp.moveaxis(coarse_out, 0, 2).reshape(
        (coarse_shape[0] // groups, coarse_shape[1], groups * coarse_shape[2])
    )
    return hidden_out[None], coarse_out[None]


def solution(mesh):
    placed = (
        P(None, "chan", "space", None),
        P("space", None),
        P("space", None),
        P("chan", None, None, None),
        P("chan"),
        P("chan", None, None, None),
        P("chan"),
    )
    return jax.shard_map(
        per_device,
        mesh=mesh,
        in_specs=placed,
        out_specs=(P(None, "chan", "space", None), P(None, "chan", "space", None)),
        check_vma=False,
    )
```

```python
import jax
import jax.numpy as jnp
from jax import lax
from jax.sharding import PartitionSpec as P


def shifted(array, axis, by):
    devices = lax.axis_size(axis)
    pairs = [(i, i + by) for i in range(devices) if 0 <= i + by < devices]
    return lax.ppermute(array, axis, pairs)


def rim_code(table, first_col, width):
    cycle = table.shape[0]
    cols = (first_col + jnp.arange(width)) % cycle
    picked = lax.dynamic_slice_in_dim(
        jnp.concatenate([table, table], axis=0), first_col % cycle, width, axis=0
    )
    code = jnp.where(picked == (cols + cycle - 1) % cycle, -1, 2)
    code = jnp.where(picked == (cols + 1) % cycle, 1, code)
    code = jnp.where(picked == cols, 0, code)
    return code.astype(jnp.bfloat16)


def apply_code(source, code):
    width = code.shape[0]
    same = source[..., 1 : width + 1]
    prev = source[..., 0:width]
    nxt = source[..., 2 : width + 2]
    zero = jnp.zeros_like(same)
    out = jnp.where(code == -1, prev, zero)
    out = jnp.where(code == 1, nxt, out)
    out = jnp.where(code == 0, same, out)
    return out


def remap_window(source, table, first_col, width):
    return apply_code(source, rim_code(table, first_col, width))


def remap_full(row, table):
    cycle = table.shape[0]
    wrapped = jnp.concatenate([row[..., -1:], row, row[..., :1]], axis=-1)
    return remap_window(wrapped, table, 0, cycle)


def split3(v):
    hi = lax.reduce_precision(v, exponent_bits=8, mantissa_bits=7)
    rest = v - hi
    mid = lax.reduce_precision(rest, exponent_bits=8, mantissa_bits=7)
    lo = rest - mid
    return jnp.stack([hi, mid, lo], -1).astype(jnp.bfloat16)


def join3(parts):
    parts = parts.astype(jnp.float32)
    return (parts[..., 0] + parts[..., 1]) + parts[..., 2]


def conv(x, w, stride):
    return lax.conv_general_dilated(
        x,
        w,
        window_strides=stride,
        padding="VALID",
        dimension_numbers=("NCHW", "HWOI", "NCHW"),
        preferred_element_type=jnp.float32,
    )


def column_windows(padded, groups, halo):
    cycle = padded.shape[-1]
    block = cycle // groups
    lead = padded.shape[:-1]
    mid = padded.reshape(lead + (groups, block))
    left = jnp.roll(mid[..., block - halo :], 1, axis=-2)
    right = jnp.roll(mid[..., :halo], -1, axis=-2)
    wins = jnp.concatenate([left, mid, right], axis=-1)
    return jnp.moveaxis(wins, -2, 0)


def gather_low_bits(part, share):
    count = lax.axis_size("space")
    me = lax.axis_index("space")
    acc = part[None]
    bit = share // 2
    while bit >= 1:
        recv = lax.ppermute(acc, "space", [(i, i ^ bit) for i in range(count)])
        low = (me & bit) == 0
        pair = jnp.where(low, jnp.stack([acc, recv], 1), jnp.stack([recv, acc], 1))
        acc = pair.reshape((-1,) + part.shape)
        bit //= 2
    return acc


def pad_to(flat, multiple):
    extra = (-flat.shape[-1]) % multiple
    return jnp.pad(flat, [(0, 0)] * (flat.ndim - 1) + [(0, extra)])


def per_device(features, top_map, bottom_map, first_weight, first_bias, second_weight, second_bias):
    groups = lax.axis_size("chan")
    me = lax.axis_index("chan")
    x = features[0]
    chans = x.shape[0]
    rows = x.shape[1]
    cycle = x.shape[2]
    block = cycle // groups
    upper_map = top_map[0]
    lower_map = bottom_map[0]
    n1 = first_weight.shape[0]
    n2 = second_weight.shape[0]

    halo = 3
    width = block + 2 * halo
    wins = column_windows(x, groups, halo + 1).reshape(groups, -1)
    feat_len = wins.shape[1]

    w1_len = first_weight.size
    w_total = w1_len + second_weight.size
    packed_w = jnp.concatenate(
        [
            jnp.transpose(first_weight, (1, 2, 0, 3)).reshape(-1),
            jnp.transpose(second_weight, (1, 2, 0, 3)).reshape(-1),
            split3(jnp.concatenate([first_bias, second_bias])).reshape(-1),
        ]
    )
    w_len = packed_w.shape[0]
    share = 4
    quarter = -(-w_len // (share * 128)) * 128
    packed_w = jnp.pad(packed_w, (0, share * quarter - w_len))
    where_me = lax.axis_index("space") % share
    mine = lax.dynamic_slice_in_dim(packed_w, where_me * quarter, quarter)
    sends = jnp.concatenate([wins, jnp.broadcast_to(mine[None], (groups, quarter))], 1)
    got = lax.all_to_all(
        pad_to(sends, 256).reshape(groups, 2, -1), "chan", 0, 0, tiled=True
    ).reshape(groups, -1)

    tile = got[:, :feat_len].reshape(groups * chans, rows, width + 2)
    pieces = gather_low_bits(got[:, feat_len : feat_len + quarter], share)
    every = jnp.moveaxis(pieces, 0, 1).reshape(groups, -1)
    k1 = first_weight.shape[1:3]
    k2 = second_weight.shape[1:3]
    w1 = every[:, :w1_len].reshape((groups,) + k1 + (n1, first_weight.shape[3]))
    w1 = jnp.moveaxis(w1, 0, 2).reshape(k1 + (groups * n1, first_weight.shape[3]))
    w2 = every[:, w1_len:w_total].reshape((groups,) + k2 + (n2, second_weight.shape[3]))
    w2 = jnp.moveaxis(w2, 0, 2).reshape(k2 + (groups * n2, second_weight.shape[3]))
    b_all = every[:, w_total:w_len].reshape(groups, n1 + n2, 3)
    b1 = join3(b_all[:, :n1]).reshape(-1)
    b2 = join3(b_all[:, n1:]).reshape(-1)

    start = me * block - halo
    lower_code = rim_code(lower_map, start, width)
    code_rows = jnp.broadcast_to(jnp.pad(lower_code, (1, 1))[None, None], (1, rows, width + 2))
    prior_ext = shifted(jnp.concatenate([tile, code_rows], 0), "space", 1)
    prior = prior_ext[: groups * chans]
    prior_code = prior_ext[groups * chans, 0, 1 : width + 1]
    below_src = shifted(tile[:, 0, :], "space", -1)
    above = remap_window(prior[:, rows - 1, :], upper_map, start, width)
    below = apply_code(below_src, lower_code)
    prior_below = apply_code(tile[:, 0, :], prior_code)
    inner = tile[:, :, 1 : width + 1]
    prior_inner = prior[:, :, 1 : width + 1]
    window = jnp.concatenate([above[:, None], inner, below[:, None]], axis=1)
    prior_window = jnp.concatenate([prior_inner, prior_below[:, None]], axis=1)

    pre1 = conv(window[None], w1, (1, 1))
    hidden_win = jax.nn.gelu(pre1 + b1[None, :, None, None]).astype(jnp.bfloat16)[0]
    pre_prior = conv(prior_window[None], w1, (1, 1))
    prior_hidden = jax.nn.gelu(pre_prior + b1[None, :, None, None]).astype(jnp.bfloat16)[0, :, 0, :]
    has_prior = lax.axis_index("space") > 0
    rim_src = jnp.where(has_prior, prior_hidden, jnp.zeros_like(prior_hidden))
    rim = remap_window(rim_src, upper_map, me * block - 1, block + 2)
    stacked = jnp.concatenate([rim[:, None], hidden_win[:, :, 1 : block + 3]], axis=1)
    pre2 = conv(stacked[None], w2, (1, 2))
    coarse_win = jax.nn.gelu(pre2 + b2[None, :, None, None]).astype(jnp.bfloat16)[0]

    hidden_part = hidden_win[:, :, halo - 1 : halo - 1 + block].reshape(groups, -1)
    coarse_part = coarse_win.reshape(groups, -1)
    back = lax.all_to_all(
        jnp.concatenate([hidden_part, coarse_part], 1).reshape(groups, 2, -1),
        "chan", 0, 0, tiled=True,
    ).reshape(groups, -1)
    h_len = hidden_part.shape[1]
    hidden_out = back[:, :h_len].reshape((groups, chans, rows, block))
    hidden_out = jnp.moveaxis(hidden_out, 0, 2).reshape(chans, rows, cycle)
    coarse_shape = coarse_win.shape
    coarse_out = back[:, h_len:].reshape(
        (groups, coarse_shape[0] // groups) + coarse_shape[1:]
    )
    coarse_out = jnp.moveaxis(coarse_out, 0, 2).reshape(
        (coarse_shape[0] // groups, coarse_shape[1], groups * coarse_shape[2])
    )
    return hidden_out[None], coarse_out[None]


def solution(mesh):
    placed = (
        P(None, "chan", "space", None),
        P("space", None),
        P("space", None),
        P("chan", None, None, None),
        P("chan"),
        P("chan", None, None, None),
        P("chan"),
    )
    return jax.shard_map(
        per_device,
        mesh=mesh,
        in_specs=placed,
        out_specs=(P(None, "chan", "space", None), P(None, "chan", "space", None)),
        check_vma=False,
    )
```

```python
import jax
import jax.numpy as jnp
from jax import lax
from jax.sharding import PartitionSpec as P


def shifted(array, axis, by):
    devices = lax.axis_size(axis)
    pairs = [(i, i + by) for i in range(devices) if 0 <= i + by < devices]
    return lax.ppermute(array, axis, pairs)


def rim_code(table, first_col, width):
    cycle = table.shape[0]
    cols = (first_col + jnp.arange(width)) % cycle
    picked = lax.dynamic_slice_in_dim(
        jnp.concatenate([table, table], axis=0), first_col % cycle, width, axis=0
    )
    code = jnp.where(picked == (cols + cycle - 1) % cycle, -1, 2)
    code = jnp.where(picked == (cols + 1) % cycle, 1, code)
    code = jnp.where(picked == cols, 0, code)
    return code.astype(jnp.bfloat16)


def apply_code(source, code):
    width = code.shape[0]
    same = source[..., 1 : width + 1]
    prev = source[..., 0:width]
    nxt = source[..., 2 : width + 2]
    zero = jnp.zeros_like(same)
    out = jnp.where(code == -1, prev, zero)
    out = jnp.where(code == 1, nxt, out)
    out = jnp.where(code == 0, same, out)
    return out


def remap_window(source, table, first_col, width):
    return apply_code(source, rim_code(table, first_col, width))


def remap_full(row, table):
    cycle = table.shape[0]
    wrapped = jnp.concatenate([row[..., -1:], row, row[..., :1]], axis=-1)
    return remap_window(wrapped, table, 0, cycle)


def split3(v):
    hi = lax.reduce_precision(v, exponent_bits=8, mantissa_bits=7)
    rest = v - hi
    mid = lax.reduce_precision(rest, exponent_bits=8, mantissa_bits=7)
    lo = rest - mid
    return jnp.stack([hi, mid, lo], -1).astype(jnp.bfloat16)


def join3(parts):
    parts = parts.astype(jnp.float32)
    return (parts[..., 0] + parts[..., 1]) + parts[..., 2]


def conv(x, w, stride):
    return lax.conv_general_dilated(
        x,
        w,
        window_strides=stride,
        padding="VALID",
        dimension_numbers=("NCHW", "HWOI", "NCHW"),
        preferred_element_type=jnp.float32,
    )


def column_windows(padded, groups, halo):
    cycle = padded.shape[-1]
    block = cycle // groups
    lead = padded.shape[:-1]
    mid = padded.reshape(lead + (groups, block))
    left = jnp.roll(mid[..., block - halo :], 1, axis=-2)
    right = jnp.roll(mid[..., :halo], -1, axis=-2)
    wins = jnp.concatenate([left, mid, right], axis=-1)
    return jnp.moveaxis(wins, -2, 0)


def gather_low_bits(part, share):
    count = lax.axis_size("space")
    me = lax.axis_index("space")
    acc = part[None]
    bit = 1
    while bit < share:
        recv = lax.ppermute(acc, "space", [(i, i ^ bit) for i in range(count)])
        low = (me & bit) == 0
        pair = jnp.where(low, jnp.stack([acc, recv], 0), jnp.stack([recv, acc], 0))
        acc = pair.reshape((-1,) + part.shape)
        bit *= 2
    return acc


def pad_to(flat, multiple):
    extra = (-flat.shape[-1]) % multiple
    return jnp.pad(flat, [(0, 0)] * (flat.ndim - 1) + [(0, extra)])


def per_device(features, top_map, bottom_map, first_weight, first_bias, second_weight, second_bias):
    groups = lax.axis_size("chan")
    me = lax.axis_index("chan")
    x = features[0]
    chans = x.shape[0]
    rows = x.shape[1]
    cycle = x.shape[2]
    block = cycle // groups
    upper_map = top_map[0]
    lower_map = bottom_map[0]
    n1 = first_weight.shape[0]
    n2 = second_weight.shape[0]

    halo = 3
    width = block + 2 * halo
    wins = column_windows(x, groups, halo + 1).reshape(groups, -1)
    feat_len = wins.shape[1]

    w1_len = first_weight.size
    w_total = w1_len + second_weight.size
    packed_w = jnp.concatenate(
        [
            jnp.transpose(first_weight, (1, 2, 0, 3)).reshape(-1),
            jnp.transpose(second_weight, (1, 2, 0, 3)).reshape(-1),
            split3(jnp.concatenate([first_bias, second_bias])).reshape(-1),
        ]
    )
    w_len = packed_w.shape[0]
    share = 4
    quarter = -(-w_len // (share * 128)) * 128
    packed_w = jnp.pad(packed_w, (0, share * quarter - w_len))
    where_me = lax.axis_index("space") % share
    mine = lax.dynamic_slice_in_dim(packed_w, where_me * quarter, quarter)
    sends = jnp.concatenate([wins, jnp.broadcast_to(mine[None], (groups, quarter))], 1)
    got = lax.all_to_all(
        pad_to(sends, 256).reshape(groups, 2, -1), "chan", 0, 0, tiled=True
    ).reshape(groups, -1)

    tile = got[:, :feat_len].reshape(groups * chans, rows, width + 2)
    pieces = gather_low_bits(got[:, feat_len : feat_len + quarter], share)
    every = jnp.moveaxis(pieces, 0, 1).reshape(groups, -1)
    k1 = first_weight.shape[1:3]
    k2 = second_weight.shape[1:3]
    w1 = every[:, :w1_len].reshape((groups,) + k1 + (n1, first_weight.shape[3]))
    w1 = jnp.moveaxis(w1, 0, 2).reshape(k1 + (groups * n1, first_weight.shape[3]))
    w2 = every[:, w1_len:w_total].reshape((groups,) + k2 + (n2, second_weight.shape[3]))
    w2 = jnp.moveaxis(w2, 0, 2).reshape(k2 + (groups * n2, second_weight.shape[3]))
    b_all = every[:, w_total:w_len].reshape(groups, n1 + n2, 3)
    b1 = join3(b_all[:, :n1]).reshape(-1)
    b2 = join3(b_all[:, n1:]).reshape(-1)

    start = me * block - halo
    lower_code = rim_code(lower_map, start, width)
    code_rows = jnp.broadcast_to(jnp.pad(lower_code, (1, 1))[None, None], (1, rows, width + 2))
    prior_ext = shifted(jnp.concatenate([tile, code_rows], 0), "space", 1)
    prior = prior_ext[: groups * chans]
    prior_code = prior_ext[groups * chans, 0, 1 : width + 1]
    below_src = shifted(tile[:, 0, :], "space", -1)
    above = remap_window(prior[:, rows - 1, :], upper_map, start, width)
    below = apply_code(below_src, lower_code)
    prior_below = apply_code(tile[:, 0, :], prior_code)
    inner = tile[:, :, 1 : width + 1]
    prior_inner = prior[:, :, 1 : width + 1]
    window = jnp.stack(
        [
            jnp.concatenate([above[:, None], inner, below[:, None]], axis=1),
            jnp.concatenate([prior_inner, prior_below[:, None], prior_below[:, None]], axis=1),
        ],
        0,
    )

    pre1 = conv(window, w1, (1, 1))
    both = jax.nn.gelu(pre1 + b1[None, :, None, None]).astype(jnp.bfloat16)
    hidden_win = both[0]
    has_prior = lax.axis_index("space") > 0
    rim_src = jnp.where(has_prior, both[1, :, 0, :], jnp.zeros_like(both[1, :, 0, :]))
    rim = remap_window(rim_src, upper_map, me * block - 1, block + 2)
    stacked = jnp.concatenate([rim[:, None], hidden_win[:, :, 1 : block + 3]], axis=1)
    pre2 = conv(stacked[None], w2, (1, 2))
    coarse_win = jax.nn.gelu(pre2 + b2[None, :, None, None]).astype(jnp.bfloat16)[0]

    hidden_part = hidden_win[:, :, halo - 1 : halo - 1 + block].reshape(groups, -1)
    coarse_part = coarse_win.reshape(groups, -1)
    back = lax.all_to_all(
        jnp.concatenate([hidden_part, coarse_part], 1).reshape(groups, 2, -1),
        "chan", 0, 0, tiled=True,
    ).reshape(groups, -1)
    h_len = hidden_part.shape[1]
    hidden_out = back[:, :h_len].reshape((groups, chans, rows, block))
    hidden_out = jnp.moveaxis(hidden_out, 0, 2).reshape(chans, rows, cycle)
    coarse_shape = coarse_win.shape
    coarse_out = back[:, h_len:].reshape(
        (groups, coarse_shape[0] // groups) + coarse_shape[1:]
    )
    coarse_out = jnp.moveaxis(coarse_out, 0, 2).reshape(
        (coarse_shape[0] // groups, coarse_shape[1], groups * coarse_shape[2])
    )
    return hidden_out[None], coarse_out[None]


def solution(mesh):
    placed = (
        P(None, "chan", "space", None),
        P("space", None),
        P("space", None),
        P("chan", None, None, None),
        P("chan"),
        P("chan", None, None, None),
        P("chan"),
    )
    return jax.shard_map(
        per_device,
        mesh=mesh,
        in_specs=placed,
        out_specs=(P(None, "chan", "space", None), P(None, "chan", "space", None)),
        check_vma=False,
    )
```
